128 devices in a mesh: group: 8 (over y, z_hi), blk: 16 (over x, z_lo, core).
Axes of the slice: x: 4, y: 4, z: 4 (z_hi: 2, z_lo: 2; z = z_hi * 2 + z_lo), core: 2. Of those that a mesh axis runs over, the one named last changes fastest.
Arguments:
- embeddings: float32 [73728, 1024], P(('group', 'blk')), may hold values from -100 to 100
- cluster: int32 [73728], P(('group', 'blk')), may hold values from 0 to 63, as said below
- global_index: int32 [73728], P(('group', 'blk')), may hold values from 0 to 73727, each once
- send_counts: int32 [128, 8], P(('group', 'blk')), may hold values from 1 to 108, as said below
Outputs:
- best_cosine: float32 [73728], P(('group', 'blk'))
The draws below stay inside these ranges and needn't reach their ends.
Inputs may be any that keep to these rules, and one draw needn't show every extreme that they name: The row's cluster group is given by send_counts; of the rows that one device sends to one cluster group, at most 7 have a cluster number in any one block c // 4 of consecutive cluster numbers, and every device has exactly 7 in some block. `global_index`: each number once over all devices. The 8 counts of a device sum to 576; its rows stand in order of cluster group, send_counts[d,g] of them for group g; every device has a count of exactly 108.
All inputs are finite; a program needn't handle non-finite values.
Results may differ from the reference program's by a relative error of at most 0.0003.
Values may be sent and summed in bfloat16 or wider, within the bound.
No kernel may reach another device: no remote copies, remote signals or barrier semaphores. Data moves between devices by JAX's collectives and lax.ppermute only.
A program may use at most 128 MiB of HBM per device.

```python
import math
import jax
import jax.numpy as jnp
from jax import lax

E = 1024
ROWS_DEV = 576
KLOC = 64
CAP = 108
IPG = 9216
TOTAL = 73728
N_GROUP = 8
N_BLK = 16
DEVICES = 128


def layout(key):
    spread = ROWS_DEV - CAP
    share = spread // (N_GROUP - 1)
    leftover = spread - share * (N_GROUP - 1)
    jitter = max(0, min(share - 1, CAP - share - 1))
    busiest = jax.random.randint(jax.random.fold_in(key, 11), (DEVICES,), 0, N_GROUP)
    raised = jax.random.randint(jax.random.fold_in(key, 12), (DEVICES, N_GROUP - 1), 0, jitter + 1)
    others = share + raised - jnp.roll(raised, -1, axis=1) + (jnp.arange(N_GROUP - 1) < leftover).astype(jnp.int32)
    column = jnp.arange(N_GROUP, dtype=jnp.int32)
    later = (column[None, :] > busiest[:, None]).astype(jnp.int32)
    pick_index = jnp.clip(column[None, :] - later, 0, N_GROUP - 2)
    counts = jnp.where(column[None, :] == busiest[:, None], CAP, jnp.take_along_axis(others, pick_index, axis=1)).astype(jnp.int32)
    cum_ends = jnp.cumsum(counts, axis=1).astype(jnp.int32)
    starts = cum_ends - counts
    position = jnp.arange(ROWS_DEV, dtype=jnp.int32)
    owner_dev = jnp.sum((position[None, :, None] >= cum_ends[:, None, :]).astype(jnp.int32), axis=2)
    in_run = position[None, :] - jnp.take_along_axis(starts, owner_dev, axis=1)
    run_keys = jax.random.split(jax.random.fold_in(key, 14), DEVICES * N_GROUP)
    orders = jax.vmap(lambda one_key: jax.random.permutation(one_key, N_BLK))(run_keys).astype(jnp.int32)
    run_row = jnp.arange(DEVICES, dtype=jnp.int32)[:, None] * N_GROUP + owner_dev
    block_of = orders[run_row.reshape(-1), (in_run % N_BLK).reshape(-1)]
    per_block = KLOC // N_BLK
    inner = jax.random.randint(jax.random.fold_in(key, 13), (TOTAL,), 0, per_block)
    cluster_ids = (block_of * per_block + inner).astype(jnp.int32)
    repeat = jax.random.randint(jax.random.fold_in(key, 15), (TOTAL,), 0, IPG // KLOC)
    item_local = cluster_ids + KLOC * repeat
    owner_group = owner_dev.reshape(-1)
    item_global = owner_group * IPG + item_local
    return (counts, owner_group, item_global, cluster_ids)


def draw_send_counts(key, part):
    return layout(key)[0]


def draw_cluster(key, part):
    return layout(key)[3]


def draw_embeddings(key, part):
    counts, owner_group, item_global, cluster_ids = layout(key)
    centers = jax.random.normal(jax.random.fold_in(key, 21), (N_GROUP * KLOC, E), jnp.float32)
    center_rows = jnp.take(centers, owner_group * KLOC + cluster_ids, axis=0)
    shared_key = jax.random.fold_in(key, 22)

    def item_normal(item_id):
        return jax.random.normal(jax.random.fold_in(shared_key, item_id), (E,), jnp.float32)
    fresh_key = jax.random.fold_in(key, 23)
    mix_weight = jnp.exp(jax.random.uniform(jax.random.fold_in(key, 24), (TOTAL, 1), jnp.float32, math.log(0.2), math.log(2.0)))
    shared = jax.vmap(item_normal)(item_global)
    fresh = jax.random.normal(fresh_key, (TOTAL, E), jnp.float32)
    row_scale = jnp.exp(jax.random.uniform(jax.random.fold_in(key, 25), (TOTAL, 1), jnp.float32, math.log(0.5), math.log(5.0)))
    values = row_scale * (mix_weight * center_rows + shared + 0.5 * fresh)
    return jnp.clip(values, -100.0, 100.0).astype(jnp.float32)


def setup_inputs(seed: int = 0) -> dict:
    arg_keys = jax.random.split(jax.random.key(seed), 5)
    embeddings = draw_embeddings(jax.random.fold_in(arg_keys[4], 71), 0)
    cluster = draw_cluster(jax.random.fold_in(arg_keys[4], 71), 0)
    global_index = jax.random.permutation(arg_keys[2], TOTAL).astype(jnp.int32)
    send_counts = draw_send_counts(jax.random.fold_in(arg_keys[4], 71), 0)
    return {"embeddings": embeddings, "cluster": cluster, "global_index": global_index, "send_counts": send_counts}


def reference(embeddings, cluster, global_index, send_counts):
    squares = lax.optimization_barrier(jnp.sum(embeddings * embeddings, axis=1, keepdims=True))
    unit_rows = (embeddings * lax.rsqrt(squares + 1e-06)).astype(jnp.bfloat16)
    cum_ends = jnp.cumsum(send_counts, axis=1).astype(jnp.int32)
    position = jnp.arange(ROWS_DEV, dtype=jnp.int32)
    owner_group = lax.optimization_barrier(jnp.sum((position[None, :, None] >= cum_ends[:, None, :]).astype(jnp.int32), axis=2)).reshape(-1)
    sort_key = (owner_group * KLOC + cluster).astype(jnp.int32)
    sort_order = jnp.argsort(sort_key, stable=True).astype(jnp.int32)
    block_rows = 512
    block_count = -(-TOTAL // block_rows)
    extra_rows = block_count * block_rows - TOTAL
    sorted_key = jnp.concatenate([sort_key[sort_order], jnp.full((extra_rows,), N_GROUP * KLOC, jnp.int32)])
    sorted_ids = jnp.concatenate([global_index[sort_order], jnp.zeros((extra_rows,), jnp.int32)])
    sorted_rows = jnp.concatenate([unit_rows[sort_order].astype(jnp.float32), jnp.zeros((extra_rows, E), jnp.float32)])

    def one_block(block_index):
        first_row = (block_index * block_rows).astype(jnp.int32)
        q_rows = lax.dynamic_slice_in_dim(sorted_rows, first_row, block_rows, 0)
        q_key = lax.dynamic_slice_in_dim(sorted_key, first_row, block_rows, 0)
        q_ids = lax.dynamic_slice_in_dim(sorted_ids, first_row, block_rows, 0)
        low_edge = jnp.searchsorted(sorted_key, q_key[0], side='left').astype(jnp.int32)
        high_edge = jnp.searchsorted(sorted_key, q_key[block_rows - 1], side='right').astype(jnp.int32)

        def scan_keys(key_block, best_now):
            key_start = (key_block * block_rows).astype(jnp.int32)
            key_rows = lax.dynamic_slice_in_dim(sorted_rows, key_start, block_rows, 0)
            key_label = lax.dynamic_slice_in_dim(sorted_key, key_start, block_rows, 0)
            key_ids = lax.dynamic_slice_in_dim(sorted_ids, key_start, block_rows, 0)
            cosine = jnp.dot(q_rows, key_rows.T, preferred_element_type=jnp.float32, precision=lax.Precision.HIGHEST)
            usable = (q_key[:, None] == key_label[None, :]) & (key_ids[None, :] < q_ids[:, None])
            return jnp.maximum(best_now, lax.optimization_barrier(jnp.max(jnp.where(usable, cosine, jnp.float32(-1.0)), axis=1)))
        start_block = (low_edge // block_rows).astype(jnp.int32)
        stop_block = ((high_edge - 1) // block_rows + 1).astype(jnp.int32)
        return lax.fori_loop(start_block, stop_block, scan_keys, jnp.full((block_rows,), -1.0, jnp.float32))
    results = lax.map(one_block, jnp.arange(block_count, dtype=jnp.int32)).reshape(-1)[:TOTAL]
    return jnp.zeros((TOTAL,), jnp.float32).at[sort_order].set(results)
```

```python
import jax
import jax.numpy as jnp
from jax import lax
from jax.sharding import PartitionSpec as P

BLOCK_WIDTH = 4
BLOCK_CAP = 7
AXES = ("group", "blk")


def on_device(embeddings, cluster, global_index, send_counts):
    row_count = embeddings.shape[0]
    blocks = lax.axis_size("blk")
    devices = lax.axis_size("group") * blocks
    slots = devices * BLOCK_CAP
    counts = send_counts[0]
    cum_ends = jnp.cumsum(counts)
    squares = jnp.sum(embeddings * embeddings, axis=1, keepdims=True)
    unit_rows = (embeddings * lax.rsqrt(squares + 1e-06)).astype(jnp.bfloat16)

    position = jnp.arange(row_count, dtype=jnp.int32)
    owner_group = jnp.sum((position[:, None] >= cum_ends[None, :]).astype(jnp.int32), axis=1)
    dest = owner_group * blocks + cluster // BLOCK_WIDTH
    earlier = (dest[:, None] == dest[None, :]) & (position[None, :] < position[:, None])
    rank = jnp.sum(earlier.astype(jnp.int32), axis=1)
    slot = dest * BLOCK_CAP + rank

    slot_ids = jnp.arange(slots, dtype=jnp.int32)
    picks = slot_ids[:, None] == slot[None, :]
    send_rows = jnp.dot(
        picks.astype(jnp.bfloat16), unit_rows, preferred_element_type=jnp.float32
    ).astype(jnp.bfloat16)
    meta = global_index * BLOCK_WIDTH + cluster % BLOCK_WIDTH
    send_meta = jnp.max(jnp.where(picks, meta[None, :], -1), axis=1)

    got_rows = lax.all_to_all(
        send_rows.reshape(devices, BLOCK_CAP, -1), AXES, 0, 0, tiled=True
    ).reshape(slots, -1)
    got_meta = lax.all_to_all(
        send_meta.reshape(devices, BLOCK_CAP), AXES, 0, 0, tiled=True
    ).reshape(slots)

    cosine = lax.dot_general(
        got_rows, got_rows, (((1,), (1,)), ((), ())), preferred_element_type=jnp.float32
    )
    got_ids = got_meta // BLOCK_WIDTH
    got_sub = got_meta % BLOCK_WIDTH
    usable = (
        (got_meta[None, :] >= 0)
        & (got_sub[:, None] == got_sub[None, :])
        & (got_ids[None, :] < got_ids[:, None])
    )
    best = jnp.max(jnp.where(usable, cosine, jnp.float32(-1.0)), axis=1)

    returned = lax.all_to_all(best.reshape(devices, BLOCK_CAP), AXES, 0, 0, tiled=True)
    return returned.reshape(slots)[slot]


def solution(mesh):
    placed = (
        P(AXES, None),
        P(AXES),
        P(AXES),
        P(AXES, None),
    )
    return jax.shard_map(
        on_device, mesh=mesh, in_specs=placed, out_specs=P(AXES), check_vma=False
    )
```

```python
import jax
import jax.numpy as jnp
from jax import lax
from jax.sharding import PartitionSpec as P

BLOCK_WIDTH = 4
BLOCK_CAP = 7
CHUNK = 8
META_W = 8
AXES = ("group", "blk")


def meta_digits(cluster, global_index):
    return (
        jnp.ones_like(cluster),
        cluster % BLOCK_WIDTH,
        global_index // 4096,
        (global_index // 64) % 64,
        global_index % 64,
    )


def on_device(embeddings, cluster, global_index, send_counts):
    row_count, feat_width = embeddings.shape
    blocks = lax.axis_size("blk")
    devices = lax.axis_size("group") * blocks
    slots = devices * CHUNK
    counts = send_counts[0]
    cum_ends = jnp.cumsum(counts)
    squares = jnp.sum(embeddings * embeddings, axis=1, keepdims=True)
    unit_rows = (embeddings * lax.rsqrt(squares + 1e-06)).astype(jnp.bfloat16)

    position = jnp.arange(row_count, dtype=jnp.int32)
    owner_group = jnp.sum((position[:, None] >= cum_ends[None, :]).astype(jnp.int32), axis=1)
    dest = owner_group * blocks + cluster // BLOCK_WIDTH
    earlier = (dest[:, None] == dest[None, :]) & (position[None, :] < position[:, None])
    rank = jnp.sum(earlier.astype(jnp.int32), axis=1)
    slot = dest * CHUNK + rank

    slot_ids = jnp.arange(slots, dtype=jnp.int32)
    picks = slot_ids[:, None] == slot[None, :]
    send_rows = jnp.dot(
        picks.astype(jnp.bfloat16), unit_rows, preferred_element_type=jnp.float32
    ).astype(jnp.bfloat16)

    offset = jnp.arange(feat_width, dtype=jnp.int32)[None, :] - rank[:, None] * META_W
    spread = jnp.zeros((row_count, feat_width), jnp.int32)
    for t, digit in enumerate(meta_digits(cluster, global_index)):
        spread = jnp.where(offset == t, digit[:, None], spread)
    to_dest = dest[:, None] == jnp.arange(devices, dtype=jnp.int32)[None, :]
    meta_rows = lax.dot_general(
        to_dest.astype(jnp.bfloat16),
        spread.astype(jnp.bfloat16),
        (((0,), (0,)), ((), ())),
        preferred_element_type=jnp.float32,
    ).astype(jnp.bfloat16)
    is_meta = jnp.arange(CHUNK) == CHUNK - 1
    send = jnp.where(
        is_meta[None, :, None],
        meta_rows[:, None, :],
        send_rows.reshape(devices, CHUNK, feat_width),
    )

    got = lax.all_to_all(send, AXES, 0, 0, tiled=True)
    got_rows = got.reshape(slots, feat_width)
    coded = got[:, CHUNK - 1, : BLOCK_CAP * META_W].astype(jnp.int32)
    coded = coded.reshape(devices, BLOCK_CAP, META_W)
    pad = ((0, 0), (0, CHUNK - BLOCK_CAP))
    got_valid = jnp.pad(coded[:, :, 0], pad).reshape(slots) > 0
    got_sub = jnp.pad(coded[:, :, 1], pad).reshape(slots)
    got_ids = jnp.pad(
        coded[:, :, 2] * 4096 + coded[:, :, 3] * 64 + coded[:, :, 4], pad
    ).reshape(slots)

    cosine = lax.dot_general(
        got_rows, got_rows, (((1,), (1,)), ((), ())), preferred_element_type=jnp.float32
    )
    usable = (
        got_valid[None, :]
        & (got_sub[:, None] == got_sub[None, :])
        & (got_ids[None, :] < got_ids[:, None])
    )
    best = jnp.max(jnp.where(usable, cosine, jnp.float32(-1.0)), axis=1)

    returned = lax.all_to_all(best.reshape(devices, CHUNK), AXES, 0, 0, tiled=True)
    return jnp.sum(jnp.where(picks, returned.reshape(slots, 1), jnp.float32(0.0)), axis=0)


def solution(mesh):
    placed = (
        P(AXES, None),
        P(AXES),
        P(AXES),
        P(AXES, None),
    )
    return jax.shard_map(
        on_device, mesh=mesh, in_specs=placed, out_specs=P(AXES), check_vma=False
    )
```

```python
import jax
import jax.numpy as jnp
from jax import lax
from jax.sharding import PartitionSpec as P

BLOCK_WIDTH = 4
BLOCK_CAP = 7
CHUNK = 8
META_W = 8
AXES = ("group", "blk")


def meta_digits(cluster, global_index):
    return (
        jnp.ones_like(cluster),
        cluster % BLOCK_WIDTH,
        global_index // 4096,
        (global_index // 64) % 64,
        global_index % 64,
    )


def on_device(embeddings, cluster, global_index, send_counts):
    row_count, feat_width = embeddings.shape
    blocks = lax.axis_size("blk")
    devices = lax.axis_size("group") * blocks
    slots = devices * CHUNK
    counts = send_counts[0]
    groups = counts.shape[0]
    upto = jnp.arange(groups)[:, None] >= jnp.arange(groups)[None, :]
    cum_ends = jnp.sum(jnp.where(upto, counts[None, :], 0), axis=1)
    squares = jnp.sum(embeddings * embeddings, axis=1, keepdims=True)
    unit_rows = (embeddings * lax.rsqrt(squares + 1e-06)).astype(jnp.bfloat16)

    position = jnp.arange(row_count, dtype=jnp.int32)
    owner_group = jnp.sum((position[:, None] >= cum_ends[None, :]).astype(jnp.int32), axis=1)
    dest = owner_group * blocks + cluster // BLOCK_WIDTH
    earlier = (dest[:, None] == dest[None, :]) & (position[None, :] < position[:, None])
    rank = jnp.sum(earlier.astype(jnp.int32), axis=1)
    slot = dest * CHUNK + rank

    offset = jnp.arange(feat_width, dtype=jnp.int32)[None, :] - rank[:, None] * META_W
    spread = jnp.zeros((row_count, feat_width), jnp.int32)
    for t, digit in enumerate(meta_digits(cluster, global_index)):
        spread = jnp.where(offset == t, digit[:, None], spread)
    slot_ids = jnp.arange(slots, dtype=jnp.int32)
    picks = slot_ids[:, None] == slot[None, :]
    meta_picks = slot_ids[:, None] == (dest * CHUNK + CHUNK - 1)[None, :]
    send = jnp.dot(
        jnp.concatenate([picks, meta_picks], axis=1).astype(jnp.bfloat16),
        jnp.concatenate([unit_rows, spread.astype(jnp.bfloat16)], axis=0),
        preferred_element_type=jnp.float32,
    ).astype(jnp.bfloat16).reshape(devices, CHUNK, feat_width)

    got = lax.all_to_all(send, AXES, 0, 0, tiled=True)
    got_rows = got.reshape(slots, feat_width)
    coded = got[:, CHUNK - 1, : BLOCK_CAP * META_W].astype(jnp.int32)
    coded = coded.reshape(devices, BLOCK_CAP, META_W)
    pad = ((0, 0), (0, CHUNK - BLOCK_CAP))
    got_valid = jnp.pad(coded[:, :, 0], pad).reshape(slots) > 0
    got_sub = jnp.pad(coded[:, :, 1], pad).reshape(slots)
    got_ids = jnp.pad(
        coded[:, :, 2] * 4096 + coded[:, :, 3] * 64 + coded[:, :, 4], pad
    ).reshape(slots)

    cosine = lax.dot_general(
        got_rows, got_rows, (((1,), (1,)), ((), ())), preferred_element_type=jnp.float32
    )
    usable = (
        got_valid[None, :]
        & (got_sub[:, None] == got_sub[None, :])
        & (got_ids[None, :] < got_ids[:, None])
    )
    best = jnp.max(jnp.where(usable, cosine, jnp.float32(-1.0)), axis=1)

    lanes = 128
    wide = jnp.pad(best.reshape(devices, CHUNK), ((0, 0), (0, lanes - CHUNK)))
    returned = lax.all_to_all(wide, AXES, 0, 0, tiled=True)[:, :CHUNK]
    return jnp.sum(jnp.where(picks, returned.reshape(slots, 1), jnp.float32(0.0)), axis=0)


def solution(mesh):
    placed = (
        P(AXES, None),
        P(AXES),
        P(AXES),
        P(AXES, None),
    )
    return jax.shard_map(
        on_device, mesh=mesh, in_specs=placed, out_specs=P(AXES), check_vma=False
    )
```

```python
import jax
import jax.numpy as jnp
from jax import lax
from jax.sharding import PartitionSpec as P

BLOCK_WIDTH = 4
BLOCK_CAP = 7
CHUNK = 8
META_DIGITS = 5
AXES = ("group", "blk")


def meta_digits(cluster, global_index):
    return (
        jnp.ones_like(cluster),
        cluster % BLOCK_WIDTH,
        global_index // 4096,
        (global_index // 64) % 64,
        global_index % 64,
    )


def on_device(embeddings, cluster, global_index, send_counts):
    row_count, feat_width = embeddings.shape
    blocks = lax.axis_size("blk")
    devices = lax.axis_size("group") * blocks
    slots = devices * CHUNK
    counts = send_counts[0]
    groups = counts.shape[0]
    upto = jnp.arange(groups)[:, None] >= jnp.arange(groups)[None, :]
    cum_ends = jnp.sum(jnp.where(upto, counts[None, :], 0), axis=1)
    squares = jnp.sum(embeddings * embeddings, axis=1, keepdims=True)
    unit_rows = (embeddings * lax.rsqrt(squares + 1e-06)).astype(jnp.bfloat16)

    position = jnp.arange(row_count, dtype=jnp.int32)
    owner_group = jnp.sum((position[:, None] >= cum_ends[None, :]).astype(jnp.int32), axis=1)
    dest = owner_group * blocks + cluster // BLOCK_WIDTH
    earlier = (dest[:, None] == dest[None, :]) & (position[None, :] < position[:, None])
    rank = jnp.sum(earlier.astype(jnp.int32), axis=1)
    slot = dest * CHUNK + rank

    slot_ids = jnp.arange(slots, dtype=jnp.int32)
    picks = slot_ids[:, None] == slot[None, :]
    send_rows = jnp.dot(
        picks.astype(jnp.bfloat16), unit_rows, preferred_element_type=jnp.float32
    ).astype(jnp.bfloat16)

    lanes = 128
    column = jnp.arange(lanes, dtype=jnp.int32)[None, :]
    spread = jnp.zeros((row_count, lanes), jnp.int32)
    for t, digit in enumerate(meta_digits(cluster, global_index)):
        spread = jnp.where(column == t * CHUNK + rank[:, None], digit[:, None], spread)
    to_dest = dest[:, None] == jnp.arange(devices, dtype=jnp.int32)[None, :]
    meta_rows = lax.dot_general(
        to_dest.astype(jnp.bfloat16),
        spread.astype(jnp.bfloat16),
        (((0,), (0,)), ((), ())),
        preferred_element_type=jnp.float32,
    ).astype(jnp.bfloat16)
    send = lax.dynamic_update_slice(
        send_rows.reshape(devices, CHUNK, feat_width),
        meta_rows.reshape(devices, 1, lanes),
        (0, CHUNK - 1, 0),
    )

    got = lax.all_to_all(send, AXES, 0, 0, tiled=True)
    got_rows = got.reshape(slots, feat_width)
    coded = got[:, CHUNK - 1, : META_DIGITS * CHUNK].astype(jnp.int32)

    def digit(t):
        return coded[:, t * CHUNK : (t + 1) * CHUNK].reshape(slots)

    got_valid = digit(0) > 0
    got_sub = digit(1)
    got_ids = digit(2) * 4096 + digit(3) * 64 + digit(4)

    cosine = lax.dot_general(
        got_rows, got_rows, (((1,), (1,)), ((), ())), preferred_element_type=jnp.float32
    )
    usable = (
        got_valid[None, :]
        & (got_sub[:, None] == got_sub[None, :])
        & (got_ids[None, :] < got_ids[:, None])
    )
    best = jnp.max(jnp.where(usable, cosine, jnp.float32(-1.0)), axis=1)

    wide = jnp.pad(best.reshape(devices, CHUNK), ((0, 0), (0, lanes - CHUNK)))
    returned = lax.all_to_all(wide, AXES, 0, 0, tiled=True)[:, :CHUNK]
    return jnp.sum(jnp.where(picks, returned.reshape(slots, 1), jnp.float32(0.0)), axis=0)


def solution(mesh):
    placed = (
        P(AXES, None),
        P(AXES),
        P(AXES),
        P(AXES, None),
    )
    return jax.shard_map(
        on_device, mesh=mesh, in_specs=placed, out_specs=P(AXES), check_vma=False
    )
```

```python
import jax
import jax.numpy as jnp
from jax import lax
from jax.sharding import PartitionSpec as P

BLOCK_WIDTH = 4
BLOCK_CAP = 7
CHUNK = 8
META_DIGITS = 5
AXES = ("group", "blk")


def meta_digits(cluster, global_index):
    return (
        jnp.ones_like(cluster),
        cluster % BLOCK_WIDTH,
        global_index // 4096,
        (global_index // 64) % 64,
        global_index % 64,
    )


def on_device(embeddings, cluster, global_index, send_counts):
    row_count, feat_width = embeddings.shape
    blocks = lax.axis_size("blk")
    devices = lax.axis_size("group") * blocks
    slots = devices * CHUNK
    counts = send_counts[0]
    groups = counts.shape[0]
    upto = jnp.arange(groups)[:, None] >= jnp.arange(groups)[None, :]
    cum_ends = jnp.sum(jnp.where(upto, counts[None, :], 0), axis=1)
    squares = jnp.sum(embeddings * embeddings, axis=1, keepdims=True)
    unit_rows = (embeddings * lax.rsqrt(squares + 1e-06)).astype(jnp.bfloat16)

    position = jnp.arange(row_count, dtype=jnp.int32)
    owner_group = jnp.sum((position[:, None] >= cum_ends[None, :]).astype(jnp.int32), axis=1)
    dest = owner_group * blocks + cluster // BLOCK_WIDTH
    earlier = (dest[:, None] == dest[None, :]) & (position[None, :] < position[:, None])
    rank = jnp.sum(earlier.astype(jnp.int32), axis=1)
    slot = dest * CHUNK + rank

    lanes = 128
    column = jnp.arange(lanes, dtype=jnp.int32)[None, :]
    spread = jnp.zeros((row_count, lanes), jnp.int32)
    for t, digit in enumerate(meta_digits(cluster, global_index)):
        spread = jnp.where(column == t * CHUNK + rank[:, None], digit[:, None], spread)
    to_dest = dest[:, None] == jnp.arange(devices, dtype=jnp.int32)[None, :]
    meta_rows = lax.dot_general(
        to_dest.astype(jnp.bfloat16),
        spread.astype(jnp.bfloat16),
        (((0,), (0,)), ((), ())),
        preferred_element_type=jnp.float32,
    ).astype(jnp.bfloat16)

    slot_ids = jnp.arange(slots, dtype=jnp.int32)
    picks = slot_ids[:, None] == slot[None, :]
    meta_picks = slot_ids[:, None] == (jnp.arange(devices, dtype=jnp.int32) * CHUNK + CHUNK - 1)[None, :]
    send = jnp.dot(
        jnp.concatenate([picks, meta_picks], axis=1).astype(jnp.bfloat16),
        jnp.concatenate(
            [unit_rows, jnp.pad(meta_rows, ((0, 0), (0, feat_width - lanes)))], axis=0
        ),
        preferred_element_type=jnp.float32,
    ).astype(jnp.bfloat16).reshape(devices, CHUNK, feat_width)

    got = lax.all_to_all(send, AXES, 0, 0, tiled=True)
    got_rows = got.reshape(slots, feat_width)
    coded = got[:, CHUNK - 1, : META_DIGITS * CHUNK].astype(jnp.int32)

    def digit(t):
        return coded[:, t * CHUNK : (t + 1) * CHUNK].reshape(slots)

    got_valid = digit(0) > 0
    got_sub = digit(1)
    got_ids = digit(2) * 4096 + digit(3) * 64 + digit(4)

    cosine = lax.dot_general(
        got_rows, got_rows, (((1,), (1,)), ((), ())), preferred_element_type=jnp.float32
    )
    usable = (
        got_valid[None, :]
        & (got_sub[:, None] == got_sub[None, :])
        & (got_ids[None, :] < got_ids[:, None])
    )
    best = jnp.max(jnp.where(usable, cosine, jnp.float32(-1.0)), axis=1)

    wide = jnp.pad(best.reshape(devices, CHUNK), ((0, 0), (0, lanes - CHUNK)))
    returned = lax.all_to_all(wide, AXES, 0, 0, tiled=True)[:, :CHUNK]
    return jnp.sum(jnp.where(picks, returned.reshape(slots, 1), jnp.float32(0.0)), axis=0)


def solution(mesh):
    placed = (
        P(AXES, None),
        P(AXES),
        P(AXES),
        P(AXES, None),
    )
    return jax.shard_map(
        on_device, mesh=mesh, in_specs=placed, out_specs=P(AXES), check_vma=False
    )
```

```python
import jax
import jax.numpy as jnp
from jax import lax
from jax.experimental import pallas as pl
from jax.experimental.pallas import tpu as pltpu
from jax.sharding import PartitionSpec as P

BLOCK_WIDTH = 4
BLOCK_CAP = 7
CHUNK = 8
META_DIGITS = 5
AXES = ("group", "blk")


def meta_digits(cluster, global_index):
    return (
        jnp.ones_like(cluster),
        cluster % BLOCK_WIDTH,
        global_index // 4096,
        (global_index // 64) % 64,
        global_index % 64,
    )


def pack_kernel(x_ref, slot_ref, meta_ref, out_ref):
    x = x_ref[...]
    squares = jnp.sum(x * x, axis=1, keepdims=True)
    unit = (x * lax.rsqrt(squares + 1e-06)).astype(jnp.bfloat16)
    slots = out_ref.shape[0]
    lanes = meta_ref.shape[1]
    slot_at = lax.broadcasted_iota(jnp.int32, (slots, slot_ref.shape[1]), 0)
    picks = (slot_at == slot_ref[...]).astype(jnp.bfloat16)
    rows = jnp.dot(picks, unit, preferred_element_type=jnp.float32)
    out_ref[...] = rows.astype(jnp.bfloat16)
    meta_at = lax.broadcasted_iota(jnp.int32, (slots, meta_ref.shape[0]), 0)
    chunk_of = lax.broadcasted_iota(jnp.int32, (slots, meta_ref.shape[0]), 1)
    meta_picks = (meta_at == chunk_of * CHUNK + CHUNK - 1).astype(jnp.bfloat16)
    meta = jnp.dot(meta_picks, meta_ref[...], preferred_element_type=jnp.float32)
    out_ref[:, :lanes] = (rows[:, :lanes] + meta).astype(jnp.bfloat16)


def pack(embeddings, slot, meta_rows, slots):
    vmem = pltpu.MemorySpace.VMEM
    return pl.pallas_call(
        pack_kernel,
        out_shape=jax.ShapeDtypeStruct((slots, embeddings.shape[1]), jnp.bfloat16),
        in_specs=[pl.BlockSpec(memory_space=vmem)] * 3,
        out_specs=pl.BlockSpec(memory_space=vmem),
        compiler_params=pltpu.CompilerParams(vmem_limit_bytes=48 * 1024 * 1024),
    )(embeddings, slot.reshape(1, -1), meta_rows)


def on_device(embeddings, cluster, global_index, send_counts):
    row_count, feat_width = embeddings.shape
    blocks = lax.axis_size("blk")
    devices = lax.axis_size("group") * blocks
    slots = devices * CHUNK
    counts = send_counts[0]
    groups = counts.shape[0]
    upto = jnp.arange(groups)[:, None] >= jnp.arange(groups)[None, :]
    cum_ends = jnp.sum(jnp.where(upto, counts[None, :], 0), axis=1)

    position = jnp.arange(row_count, dtype=jnp.int32)
    owner_group = jnp.sum((position[:, None] >= cum_ends[None, :]).astype(jnp.int32), axis=1)
    dest = owner_group * blocks + cluster // BLOCK_WIDTH
    earlier = (dest[:, None] == dest[None, :]) & (position[None, :] < position[:, None])
    rank = jnp.sum(earlier.astype(jnp.int32), axis=1)
    slot = dest * CHUNK + rank

    lanes = 128
    column = jnp.arange(lanes, dtype=jnp.int32)[None, :]
    spread = jnp.zeros((row_count, lanes), jnp.int32)
    for t, digit in enumerate(meta_digits(cluster, global_index)):
        spread = jnp.where(column == t * CHUNK + rank[:, None], digit[:, None], spread)
    to_dest = dest[:, None] == jnp.arange(devices, dtype=jnp.int32)[None, :]
    meta_rows = lax.dot_general(
        to_dest.astype(jnp.bfloat16),
        spread.astype(jnp.bfloat16),
        (((0,), (0,)), ((), ())),
        preferred_element_type=jnp.float32,
    ).astype(jnp.bfloat16)

    send = pack(embeddings, slot, meta_rows, slots).reshape(devices, CHUNK, feat_width)
    slot_ids = jnp.arange(slots, dtype=jnp.int32)
    picks = slot_ids[:, None] == slot[None, :]

    got = lax.all_to_all(send, AXES, 0, 0, tiled=True)
    got_rows = got.reshape(slots, feat_width)
    coded = got[:, CHUNK - 1, : META_DIGITS * CHUNK].astype(jnp.int32)

    def digit(t):
        return coded[:, t * CHUNK : (t + 1) * CHUNK].reshape(slots)

    got_valid = digit(0) > 0
    got_sub = digit(1)
    got_ids = digit(2) * 4096 + digit(3) * 64 + digit(4)

    cosine = lax.dot_general(
        got_rows, got_rows, (((1,), (1,)), ((), ())), preferred_element_type=jnp.float32
    )
    usable = (
        got_valid[None, :]
        & (got_sub[:, None] == got_sub[None, :])
        & (got_ids[None, :] < got_ids[:, None])
    )
    best = jnp.max(jnp.where(usable, cosine, jnp.float32(-1.0)), axis=1)

    wide = jnp.pad(best.reshape(devices, CHUNK), ((0, 0), (0, lanes - CHUNK)))
    returned = lax.all_to_all(wide, AXES, 0, 0, tiled=True)[:, :CHUNK]
    return jnp.sum(jnp.where(picks, returned.reshape(slots, 1), jnp.float32(0.0)), axis=0)


def solution(mesh):
    placed = (
        P(AXES, None),
        P(AXES),
        P(AXES),
        P(AXES, None),
    )
    return jax.shard_map(
        on_device, mesh=mesh, in_specs=placed, out_specs=P(AXES), check_vma=False
    )
```

```python
import jax
import jax.numpy as jnp
from jax import lax
from jax.experimental import pallas as pl
from jax.experimental.pallas import tpu as pltpu
from jax.sharding import PartitionSpec as P

BLOCK_WIDTH = 4
BLOCK_CAP = 7
CHUNK = 8
META_DIGITS = 5
AXES = ("group", "blk")
LANES = 128


def meta_digits(cluster, global_index):
    return (
        jnp.ones_like(cluster),
        cluster % BLOCK_WIDTH,
        global_index // 4096,
        (global_index // 64) % 64,
        global_index % 64,
    )


def pack_kernel(x_hbm, idx_ref, cols_ref, out_ref, x_buf, unit_buf, sems):
    pieces = sems.shape[0]
    piece = x_buf.shape[0] // pieces
    copies = [
        pltpu.make_async_copy(
            x_hbm.at[pl.ds(j * piece, piece)], x_buf.at[pl.ds(j * piece, piece)], sems.at[j]
        )
        for j in range(pieces)
    ]
    for copy in copies:
        copy.start()
    for j, copy in enumerate(copies):
        copy.wait()
        x = x_buf[pl.ds(j * piece, piece), :]
        squares = jnp.sum(x * x, axis=1, keepdims=True)
        unit_buf[pl.ds(j * piece, piece), :] = (x * lax.rsqrt(squares + 1e-06)).astype(jnp.bfloat16)

    row_count = x_buf.shape[0]
    slots = out_ref.shape[0]
    devices = slots // CHUNK
    lanes = 128
    slot_at = lax.broadcasted_iota(jnp.int32, (slots, row_count), 0)
    picks = (slot_at == idx_ref[0:1, :]).astype(jnp.bfloat16)
    rows = jnp.dot(picks, unit_buf[...], preferred_element_type=jnp.float32)

    dest_at = lax.broadcasted_iota(jnp.int32, (devices, row_count), 0)
    to_dest = (dest_at == idx_ref[1:2, :]).astype(jnp.bfloat16)
    cols = cols_ref[...]
    column = lax.broadcasted_iota(jnp.int32, (row_count, lanes), 1)
    spread = jnp.zeros((row_count, lanes), jnp.int32)
    for t in range(META_DIGITS):
        spread = jnp.where(column == t * CHUNK + cols[:, 0:1], cols[:, t + 1 : t + 2], spread)
    meta_rows = jnp.dot(to_dest, spread.astype(jnp.bfloat16), preferred_element_type=jnp.float32)
    meta_at = lax.broadcasted_iota(jnp.int32, (slots, devices), 0)
    chunk_of = lax.broadcasted_iota(jnp.int32, (slots, devices), 1)
    meta_picks = (meta_at == chunk_of * CHUNK + CHUNK - 1).astype(jnp.bfloat16)
    meta = jnp.dot(meta_picks, meta_rows.astype(jnp.bfloat16), preferred_element_type=jnp.float32)
    out_ref[...] = rows.astype(jnp.bfloat16)
    out_ref[:, :lanes] = (rows[:, :lanes] + meta).astype(jnp.bfloat16)


def pack(embeddings, slot, dest, rank, digits, slots):
    row_count, feat_width = embeddings.shape
    vmem = pltpu.MemorySpace.VMEM
    unused = jnp.zeros_like(slot)
    index_rows = jnp.stack([slot, dest] + [unused] * 6, axis=0)
    cols = jnp.stack([rank, *digits] + [unused] * (7 - len(digits)), axis=1)
    return pl.pallas_call(
        pack_kernel,
        out_shape=jax.ShapeDtypeStruct((slots, feat_width), jnp.bfloat16),
        in_specs=[
            pl.BlockSpec(memory_space=pl.ANY),
            pl.BlockSpec(memory_space=vmem),
            pl.BlockSpec(memory_space=vmem),
        ],
        out_specs=pl.BlockSpec(memory_space=vmem),
        scratch_shapes=[
            pltpu.VMEM((row_count, feat_width), jnp.float32),
            pltpu.VMEM((row_count, feat_width), jnp.bfloat16),
            pltpu.SemaphoreType.DMA((4,)),
        ],
        compiler_params=pltpu.CompilerParams(vmem_limit_bytes=48 * 1024 * 1024),
    )(embeddings, index_rows, cols)


def on_device(embeddings, cluster, global_index, send_counts):
    row_count, feat_width = embeddings.shape
    blocks = lax.axis_size("blk")
    devices = lax.axis_size("group") * blocks
    slots = devices * CHUNK
    counts = send_counts[0]
    groups = counts.shape[0]
    upto = jnp.arange(groups)[:, None] >= jnp.arange(groups)[None, :]
    cum_ends = jnp.sum(jnp.where(upto, counts[None, :], 0), axis=1)

    position = jnp.arange(row_count, dtype=jnp.int32)
    owner_group = jnp.sum((position[:, None] >= cum_ends[None, :]).astype(jnp.int32), axis=1)
    dest = owner_group * blocks + cluster // BLOCK_WIDTH
    earlier = (dest[:, None] == dest[None, :]) & (position[None, :] < position[:, None])
    rank = jnp.sum(earlier.astype(jnp.int32), axis=1)
    slot = dest * CHUNK + rank

    send = pack(
        embeddings, slot, dest, rank, meta_digits(cluster, global_index), slots
    ).reshape(devices, CHUNK, feat_width)
    slot_ids = jnp.arange(slots, dtype=jnp.int32)
    picks = slot_ids[:, None] == slot[None, :]

    got = lax.all_to_all(send, AXES, 0, 0, tiled=True)
    got_rows = got.reshape(slots, feat_width)
    coded = got[:, CHUNK - 1, : META_DIGITS * CHUNK].astype(jnp.int32)

    def digit(t):
        return coded[:, t * CHUNK : (t + 1) * CHUNK].reshape(slots)

    got_valid = digit(0) > 0
    got_sub = digit(1)
    got_ids = digit(2) * 4096 + digit(3) * 64 + digit(4)

    cosine = lax.dot_general(
        got_rows, got_rows, (((1,), (1,)), ((), ())), preferred_element_type=jnp.float32
    )
    usable = (
        got_valid[None, :]
        & (got_sub[:, None] == got_sub[None, :])
        & (got_ids[None, :] < got_ids[:, None])
    )
    best = jnp.max(jnp.where(usable, cosine, jnp.float32(-1.0)), axis=1)

    wide = jnp.pad(best.reshape(devices, CHUNK), ((0, 0), (0, LANES - CHUNK)))
    returned = lax.all_to_all(wide, AXES, 0, 0, tiled=True)[:, :CHUNK]
    return jnp.sum(jnp.where(picks, returned.reshape(slots, 1), jnp.float32(0.0)), axis=0)


def solution(mesh):
    placed = (
        P(AXES, None),
        P(AXES),
        P(AXES),
        P(AXES, None),
    )
    return jax.shard_map(
        on_device, mesh=mesh, in_specs=placed, out_specs=P(AXES), check_vma=False
    )
```

```python
import jax
import jax.numpy as jnp
from jax import lax
from jax.experimental import pallas as pl
from jax.experimental.pallas import tpu as pltpu
from jax.sharding import PartitionSpec as P

BLOCK_WIDTH = 4
BLOCK_CAP = 7
CHUNK = 8
META_DIGITS = 5
AXES = ("group", "blk")
LANES = 128


def meta_digits(cluster, global_index):
    return (
        jnp.ones_like(cluster),
        cluster % BLOCK_WIDTH,
        global_index // 4096,
        (global_index // 64) % 64,
        global_index % 64,
    )


def pack_kernel(x_ref, idx_ref, cols_ref, out_ref):
    x = x_ref[...]
    squares = jnp.sum(x * x, axis=1, keepdims=True)
    unit = (x * lax.rsqrt(squares + 1e-06)).astype(jnp.bfloat16)
    row_count = x_ref.shape[0]
    slots = out_ref.shape[0]
    slot_at = lax.broadcasted_iota(jnp.int32, (slots, row_count), 0)
    picks = (slot_at == idx_ref[0:1, :]).astype(jnp.bfloat16)
    rows = jnp.dot(picks, unit, preferred_element_type=jnp.float32)
    out_ref[...] = rows.astype(jnp.bfloat16)

    cols = cols_ref[...]
    column = lax.broadcasted_iota(jnp.int32, (row_count, LANES), 1)
    spread = jnp.zeros((row_count, LANES), jnp.int32)
    for t in range(META_DIGITS):
        spread = jnp.where(column == t * CHUNK + cols[:, 0:1], cols[:, t + 1 : t + 2], spread)
    meta_picks = (slot_at == idx_ref[1:2, :]).astype(jnp.bfloat16)
    meta = jnp.dot(meta_picks, spread.astype(jnp.bfloat16), preferred_element_type=jnp.float32)
    out_ref[:, :LANES] = (rows[:, :LANES] + meta).astype(jnp.bfloat16)


def pack(embeddings, slot, meta_slot, rank, digits, slots):
    row_count, feat_width = embeddings.shape
    vmem = pltpu.MemorySpace.VMEM
    unused = jnp.zeros_like(slot)
    index_rows = jnp.stack([slot, meta_slot] + [unused] * 6, axis=0)
    cols = jnp.stack([rank, *digits] + [unused] * (7 - len(digits)), axis=1)
    return pl.pallas_call(
        pack_kernel,
        out_shape=jax.ShapeDtypeStruct((slots, feat_width), jnp.bfloat16),
        in_specs=[pl.BlockSpec(memory_space=vmem)] * 3,
        out_specs=pl.BlockSpec(memory_space=vmem),
        compiler_params=pltpu.CompilerParams(vmem_limit_bytes=48 * 1024 * 1024),
    )(embeddings, index_rows, cols)


def on_device(embeddings, cluster, global_index, send_counts):
    row_count, feat_width = embeddings.shape
    blocks = lax.axis_size("blk")
    devices = lax.axis_size("group") * blocks
    slots = devices * CHUNK
    counts = send_counts[0]
    groups = counts.shape[0]
    upto = jnp.arange(groups)[:, None] >= jnp.arange(groups)[None, :]
    cum_ends = jnp.sum(jnp.where(upto, counts[None, :], 0), axis=1)

    position = jnp.arange(row_count, dtype=jnp.int32)
    owner_group = jnp.sum((position[:, None] >= cum_ends[None, :]).astype(jnp.int32), axis=1)
    dest = owner_group * blocks + cluster // BLOCK_WIDTH
    earlier = (dest[:, None] == dest[None, :]) & (position[None, :] < position[:, None])
    rank = jnp.sum(earlier.astype(jnp.int32), axis=1)
    slot = dest * CHUNK + rank

    send = pack(
        embeddings, slot, dest * CHUNK + CHUNK - 1, rank, meta_digits(cluster, global_index), slots
    ).reshape(devices, CHUNK, feat_width)
    slot_ids = jnp.arange(slots, dtype=jnp.int32)
    picks = slot_ids[:, None] == slot[None, :]

    got = lax.all_to_all(send, AXES, 0, 0, tiled=True)
    got_rows = got.reshape(slots, feat_width)
    coded = got[:, CHUNK - 1, : META_DIGITS * CHUNK].astype(jnp.int32)

    def digit(t):
        return coded[:, t * CHUNK : (t + 1) * CHUNK].reshape(slots)

    got_valid = digit(0) > 0
    got_sub = digit(1)
    got_ids = digit(2) * 4096 + digit(3) * 64 + digit(4)

    cosine = lax.dot_general(
        got_rows, got_rows, (((1,), (1,)), ((), ())), preferred_element_type=jnp.float32
    )
    usable = (
        got_valid[None, :]
        & (got_sub[:, None] == got_sub[None, :])
        & (got_ids[None, :] < got_ids[:, None])
    )
    best = jnp.max(jnp.where(usable, cosine, jnp.float32(-1.0)), axis=1)

    wide = jnp.pad(best.reshape(devices, CHUNK), ((0, 0), (0, LANES - CHUNK)))
    returned = lax.all_to_all(wide, AXES, 0, 0, tiled=True)[:, :CHUNK]
    return jnp.sum(jnp.where(picks, returned.reshape(slots, 1), jnp.float32(0.0)), axis=0)


def solution(mesh):
    placed = (
        P(AXES, None),
        P(AXES),
        P(AXES),
        P(AXES, None),
    )
    return jax.shard_map(
        on_device, mesh=mesh, in_specs=placed, out_specs=P(AXES), check_vma=False
    )
```

```python
import functools

import jax
import jax.numpy as jnp
from jax import lax
from jax.experimental import pallas as pl
from jax.experimental.pallas import tpu as pltpu
from jax.sharding import PartitionSpec as P

BLOCK_WIDTH = 4
BLOCK_CAP = 7
CHUNK = 8
META_DIGITS = 5
AXES = ("group", "blk")
LANES = 128


def pack_kernel(blocks, counts_ref, cl_row_ref, cl_col_ref, gi_col_ref, x_ref, out_ref, slot_ref):
    row_count = x_ref.shape[0]
    slots = out_ref.shape[0]
    pos_row = lax.broadcasted_iota(jnp.int32, (1, row_count), 1)
    pos_col = lax.broadcasted_iota(jnp.int32, (row_count, 1), 0)
    owner_row = jnp.zeros((1, row_count), jnp.int32)
    owner_col = jnp.zeros((row_count, 1), jnp.int32)
    end = counts_ref[0]
    for g in range(1, counts_ref.shape[0] + 1):
        owner_row = owner_row + (pos_row >= end).astype(jnp.int32)
        owner_col = owner_col + (pos_col >= end).astype(jnp.int32)
        if g < counts_ref.shape[0]:
            end = end + counts_ref[g]
    cl_row = cl_row_ref[...]
    cl_col = cl_col_ref[...]
    dest_row = owner_row * blocks + lax.shift_right_logical(cl_row, 2)
    dest_col = owner_col * blocks + lax.shift_right_logical(cl_col, 2)
    same = dest_col == dest_row
    rank_row = jnp.sum((same & (pos_col < pos_row)).astype(jnp.int32), axis=0, keepdims=True)
    rank_col = jnp.sum((same & (pos_row < pos_col)).astype(jnp.int32), axis=1, keepdims=True)
    slot_row = dest_row * CHUNK + rank_row
    slot_ref[...] = slot_row

    x = x_ref[...]
    squares = jnp.sum(x * x, axis=1, keepdims=True)
    unit = (x * lax.rsqrt(squares + 1e-06)).astype(jnp.bfloat16)
    slot_at = lax.broadcasted_iota(jnp.int32, (slots, row_count), 0)
    picks = (slot_at == slot_row).astype(jnp.bfloat16)
    rows = jnp.dot(picks, unit, preferred_element_type=jnp.float32)
    out_ref[...] = rows.astype(jnp.bfloat16)

    gi_col = gi_col_ref[...]
    digits = (
        jnp.ones_like(cl_col),
        cl_col & (BLOCK_WIDTH - 1),
        lax.shift_right_logical(gi_col, 12),
        lax.shift_right_logical(gi_col, 6) & 63,
        gi_col & 63,
    )
    column = lax.broadcasted_iota(jnp.int32, (row_count, LANES), 1)
    spread = jnp.zeros((row_count, LANES), jnp.int32)
    for t, digit in enumerate(digits):
        spread = jnp.where(column == t * CHUNK + rank_col, digit, spread)
    meta_picks = (slot_at == dest_row * CHUNK + CHUNK - 1).astype(jnp.bfloat16)
    meta = jnp.dot(meta_picks, spread.astype(jnp.bfloat16), preferred_element_type=jnp.float32)
    out_ref[:, :LANES] = (rows[:, :LANES] + meta).astype(jnp.bfloat16)


def pack(embeddings, cluster, global_index, counts, blocks, slots):
    row_count, feat_width = embeddings.shape
    vmem = pltpu.MemorySpace.VMEM
    return pl.pallas_call(
        functools.partial(pack_kernel, blocks),
        out_shape=(
            jax.ShapeDtypeStruct((slots, feat_width), jnp.bfloat16),
            jax.ShapeDtypeStruct((1, row_count), jnp.int32),
        ),
        in_specs=[pl.BlockSpec(memory_space=pltpu.MemorySpace.SMEM)]
        + [pl.BlockSpec(memory_space=vmem)] * 4,
        out_specs=(pl.BlockSpec(memory_space=vmem), pl.BlockSpec(memory_space=vmem)),
        compiler_params=pltpu.CompilerParams(vmem_limit_bytes=48 * 1024 * 1024),
    )(
        counts,
        cluster.reshape(1, row_count),
        cluster.reshape(row_count, 1),
        global_index.reshape(row_count, 1),
        embeddings,
    )


def on_device(embeddings, cluster, global_index, send_counts):
    row_count, feat_width = embeddings.shape
    blocks = lax.axis_size("blk")
    devices = lax.axis_size("group") * blocks
    slots = devices * CHUNK
    send, slot = pack(embeddings, cluster, global_index, send_counts[0], blocks, slots)
    send = send.reshape(devices, CHUNK, feat_width)
    slot_ids = jnp.arange(slots, dtype=jnp.int32)
    picks = slot_ids[:, None] == slot

    got = lax.all_to_all(send, AXES, 0, 0, tiled=True)
    got_rows = got.reshape(slots, feat_width)
    coded = got[:, CHUNK - 1, : META_DIGITS * CHUNK].astype(jnp.int32)

    def digit(t):
        return coded[:, t * CHUNK : (t + 1) * CHUNK].reshape(slots)

    got_valid = digit(0) > 0
    got_sub = digit(1)
    got_ids = digit(2) * 4096 + digit(3) * 64 + digit(4)

    cosine = lax.dot_general(
        got_rows, got_rows, (((1,), (1,)), ((), ())), preferred_element_type=jnp.float32
    )
    usable = (
        got_valid[None, :]
        & (got_sub[:, None] == got_sub[None, :])
        & (got_ids[None, :] < got_ids[:, None])
    )
    best = jnp.max(jnp.where(usable, cosine, jnp.float32(-1.0)), axis=1)

    wide = jnp.pad(best.reshape(devices, CHUNK), ((0, 0), (0, LANES - CHUNK)))
    returned = lax.all_to_all(wide, AXES, 0, 0, tiled=True)[:, :CHUNK]
    return jnp.sum(jnp.where(picks, returned.reshape(slots, 1), jnp.float32(0.0)), axis=0)


def solution(mesh):
    placed = (
        P(AXES, None),
        P(AXES),
        P(AXES),
        P(AXES, None),
    )
    return jax.shard_map(
        on_device, mesh=mesh, in_specs=placed, out_specs=P(AXES), check_vma=False
    )
```

```python
import functools

import jax
import jax.numpy as jnp
from jax import lax
from jax.experimental import pallas as pl
from jax.experimental.pallas import tpu as pltpu
from jax.sharding import PartitionSpec as P

BLOCK_WIDTH = 4
BLOCK_CAP = 7
CHUNK = 8
META_DIGITS = 5
AXES = ("group", "blk")
LANES = 128


def pack_kernel(blocks, counts_ref, cl_ref, gi_ref, x_ref, out_ref, slot_ref):
    row_count = x_ref.shape[0]
    slots = out_ref.shape[0]
    pos_row = lax.broadcasted_iota(jnp.int32, (1, row_count), 1)
    pos_col = lax.broadcasted_iota(jnp.int32, (row_count, 1), 0)
    owner_row = jnp.zeros((1, row_count), jnp.int32)
    owner_col = jnp.zeros((row_count, 1), jnp.int32)
    end = counts_ref[0]
    for g in range(1, counts_ref.shape[0] + 1):
        owner_row = owner_row + (pos_row >= end).astype(jnp.int32)
        owner_col = owner_col + (pos_col >= end).astype(jnp.int32)
        if g < counts_ref.shape[0]:
            end = end + counts_ref[g]
    on_diag = pos_col == pos_row
    cl_row = cl_ref[...].reshape(1, row_count)
    gi_row = gi_ref[...].reshape(1, row_count)
    cl_col = jnp.sum(jnp.where(on_diag, cl_row, 0), axis=1, keepdims=True)
    gi_col = jnp.sum(jnp.where(on_diag, gi_row, 0), axis=1, keepdims=True)
    dest_row = owner_row * blocks + lax.shift_right_logical(cl_row, 2)
    dest_col = owner_col * blocks + lax.shift_right_logical(cl_col, 2)
    same = dest_col == dest_row
    rank_row = jnp.sum((same & (pos_col < pos_row)).astype(jnp.int32), axis=0, keepdims=True)
    rank_col = jnp.sum((same & (pos_row < pos_col)).astype(jnp.int32), axis=1, keepdims=True)
    slot_row = dest_row * CHUNK + rank_row
    slot_ref[...] = slot_row

    x = x_ref[...]
    squares = jnp.sum(x * x, axis=1, keepdims=True)
    unit = (x * lax.rsqrt(squares + 1e-06)).astype(jnp.bfloat16)
    slot_at = lax.broadcasted_iota(jnp.int32, (slots, row_count), 0)
    picks = (slot_at == slot_row).astype(jnp.bfloat16)
    rows = jnp.dot(picks, unit, preferred_element_type=jnp.float32)
    out_ref[...] = rows.astype(jnp.bfloat16)

    digits = (
        jnp.ones_like(cl_col),
        cl_col & (BLOCK_WIDTH - 1),
        lax.shift_right_logical(gi_col, 12),
        lax.shift_right_logical(gi_col, 6) & 63,
        gi_col & 63,
    )
    column = lax.broadcasted_iota(jnp.int32, (row_count, LANES), 1)
    spread = jnp.zeros((row_count, LANES), jnp.int32)
    for t, digit in enumerate(digits):
        spread = jnp.where(column == t * CHUNK + rank_col, digit, spread)
    meta_picks = (slot_at == dest_row * CHUNK + CHUNK - 1).astype(jnp.bfloat16)
    meta = jnp.dot(meta_picks, spread.astype(jnp.bfloat16), preferred_element_type=jnp.float32)
    out_ref[:, :LANES] = (rows[:, :LANES] + meta).astype(jnp.bfloat16)


def pack(embeddings, cluster, global_index, counts, blocks, slots):
    row_count, feat_width = embeddings.shape
    vmem = pltpu.MemorySpace.VMEM
    return pl.pallas_call(
        functools.partial(pack_kernel, blocks),
        out_shape=(
            jax.ShapeDtypeStruct((slots, feat_width), jnp.bfloat16),
            jax.ShapeDtypeStruct((1, row_count), jnp.int32),
        ),
        in_specs=[pl.BlockSpec(memory_space=pltpu.MemorySpace.SMEM)]
        + [pl.BlockSpec(memory_space=vmem)] * 3,
        out_specs=(pl.BlockSpec(memory_space=vmem), pl.BlockSpec(memory_space=vmem)),
        compiler_params=pltpu.CompilerParams(vmem_limit_bytes=48 * 1024 * 1024),
    )(
        counts,
        cluster,
        global_index,
        embeddings,
    )


def on_device(embeddings, cluster, global_index, send_counts):
    row_count, feat_width = embeddings.shape
    blocks = lax.axis_size("blk")
    devices = lax.axis_size("group") * blocks
    slots = devices * CHUNK
    send, slot = pack(embeddings, cluster, global_index, send_counts[0], blocks, slots)
    send = send.reshape(devices, CHUNK, feat_width)
    slot_ids = jnp.arange(slots, dtype=jnp.int32)
    picks = slot_ids[:, None] == slot

    got = lax.all_to_all(send, AXES, 0, 0, tiled=True)
    got_rows = got.reshape(slots, feat_width)
    coded = got[:, CHUNK - 1, : META_DIGITS * CHUNK].astype(jnp.int32)

    def digit(t):
        return coded[:, t * CHUNK : (t + 1) * CHUNK].reshape(slots)

    got_valid = digit(0) > 0
    got_sub = digit(1)
    got_ids = digit(2) * 4096 + digit(3) * 64 + digit(4)

    cosine = lax.dot_general(
        got_rows, got_rows, (((1,), (1,)), ((), ())), preferred_element_type=jnp.float32
    )
    usable = (
        got_valid[None, :]
        & (got_sub[:, None] == got_sub[None, :])
        & (got_ids[None, :] < got_ids[:, None])
    )
    best = jnp.max(jnp.where(usable, cosine, jnp.float32(-1.0)), axis=1)

    wide = jnp.pad(best.reshape(devices, CHUNK), ((0, 0), (0, LANES - CHUNK)))
    returned = lax.all_to_all(wide, AXES, 0, 0, tiled=True)[:, :CHUNK]
    return jnp.sum(jnp.where(picks, returned.reshape(slots, 1), jnp.float32(0.0)), axis=0)


def solution(mesh):
    placed = (
        P(AXES, None),
        P(AXES),
        P(AXES),
        P(AXES, None),
    )
    return jax.shard_map(
        on_device, mesh=mesh, in_specs=placed, out_specs=P(AXES), check_vma=False
    )
```

```python
import jax
import jax.numpy as jnp
from jax import lax
from jax.experimental import pallas as pl
from jax.experimental.pallas import tpu as pltpu
from jax.sharding import PartitionSpec as P

BLOCK_WIDTH = 4
BLOCK_CAP = 7
CHUNK = 8
META_DIGITS = 5
AXES = ("group", "blk")
LANES = 128


def meta_digits(cluster, global_index):
    return (
        jnp.ones_like(cluster),
        cluster % BLOCK_WIDTH,
        global_index // 4096,
        (global_index // 64) % 64,
        global_index % 64,
    )


def pack_kernel(x_ref, idx_ref, cols_ref, out_ref):
    x = x_ref[...]
    squares = jnp.sum(x * x, axis=1, keepdims=True)
    unit = (x * lax.rsqrt(squares + 1e-06)).astype(jnp.bfloat16)
    row_count = x_ref.shape[0]
    slots = out_ref.shape[0]
    slot_at = lax.broadcasted_iota(jnp.int32, (slots, row_count), 0)
    picks = (slot_at == idx_ref[0:1, :]).astype(jnp.bfloat16)
    rows = jnp.dot(picks, unit, preferred_element_type=jnp.float32)
    out_ref[...] = rows.astype(jnp.bfloat16)

    cols = cols_ref[...]
    column = lax.broadcasted_iota(jnp.int32, (row_count, LANES), 1)
    spread = jnp.zeros((row_count, LANES), jnp.int32)
    for t in range(META_DIGITS):
        spread = jnp.where(column == t * CHUNK + cols[:, 0:1], cols[:, t + 1 : t + 2], spread)
    meta_picks = (slot_at == idx_ref[1:2, :]).astype(jnp.bfloat16)
    meta = jnp.dot(meta_picks, spread.astype(jnp.bfloat16), preferred_element_type=jnp.float32)
    out_ref[:, :LANES] = (rows[:, :LANES] + meta).astype(jnp.bfloat16)


def pack(embeddings, slot, meta_slot, rank, digits, slots):
    row_count, feat_width = embeddings.shape
    vmem = pltpu.MemorySpace.VMEM
    unused = jnp.zeros_like(slot)
    index_rows = jnp.stack([slot, meta_slot] + [unused] * 6, axis=0)
    cols = jnp.stack([rank, *digits] + [unused] * (7 - len(digits)), axis=1)
    return pl.pallas_call(
        pack_kernel,
        out_shape=jax.ShapeDtypeStruct((slots, feat_width), jnp.bfloat16),
        in_specs=[pl.BlockSpec(memory_space=vmem)] * 3,
        out_specs=pl.BlockSpec(memory_space=vmem),
        compiler_params=pltpu.CompilerParams(vmem_limit_bytes=48 * 1024 * 1024),
    )(embeddings, index_rows, cols)


def on_device(embeddings, cluster, global_index, send_counts):
    row_count, feat_width = embeddings.shape
    blocks = lax.axis_size("blk")
    devices = lax.axis_size("group") * blocks
    slots = devices * CHUNK
    small = lax.optimization_barrier(
        jnp.concatenate([cluster, global_index, send_counts[0]])
    )
    cluster = small[:row_count]
    global_index = small[row_count : 2 * row_count]
    counts = small[2 * row_count :]
    groups = counts.shape[0]
    upto = jnp.arange(groups)[:, None] >= jnp.arange(groups)[None, :]
    cum_ends = jnp.sum(jnp.where(upto, counts[None, :], 0), axis=1)

    position = jnp.arange(row_count, dtype=jnp.int32)
    owner_group = jnp.sum((position[:, None] >= cum_ends[None, :]).astype(jnp.int32), axis=1)
    dest = owner_group * blocks + cluster // BLOCK_WIDTH
    earlier = (dest[:, None] == dest[None, :]) & (position[None, :] < position[:, None])
    rank = jnp.sum(earlier.astype(jnp.int32), axis=1)
    slot = dest * CHUNK + rank

    send = pack(
        embeddings, slot, dest * CHUNK + CHUNK - 1, rank, meta_digits(cluster, global_index), slots
    ).reshape(devices, CHUNK, feat_width)
    slot_ids = jnp.arange(slots, dtype=jnp.int32)
    picks = slot_ids[:, None] == slot[None, :]

    got = lax.all_to_all(send, AXES, 0, 0, tiled=True)
    got_rows = got.reshape(slots, feat_width)
    coded = got[:, CHUNK - 1, : META_DIGITS * CHUNK].astype(jnp.int32)

    def digit(t):
        return coded[:, t * CHUNK : (t + 1) * CHUNK].reshape(slots)

    got_valid = digit(0) > 0
    got_sub = digit(1)
    got_ids = digit(2) * 4096 + digit(3) * 64 + digit(4)

    cosine = lax.dot_general(
        got_rows, got_rows, (((1,), (1,)), ((), ())), preferred_element_type=jnp.float32
    )
    usable = (
        got_valid[None, :]
        & (got_sub[:, None] == got_sub[None, :])
        & (got_ids[None, :] < got_ids[:, None])
    )
    best = jnp.max(jnp.where(usable, cosine, jnp.float32(-1.0)), axis=1)

    wide = jnp.pad(best.reshape(devices, CHUNK), ((0, 0), (0, LANES - CHUNK)))
    returned = lax.all_to_all(wide, AXES, 0, 0, tiled=True)[:, :CHUNK]
    return jnp.sum(jnp.where(picks, returned.reshape(slots, 1), jnp.float32(0.0)), axis=0)


def solution(mesh):
    placed = (
        P(AXES, None),
        P(AXES),
        P(AXES),
        P(AXES, None),
    )
    return jax.shard_map(
        on_device, mesh=mesh, in_specs=placed, out_specs=P(AXES), check_vma=False
    )
```

```python
import jax
import jax.numpy as jnp
from jax import lax
from jax.experimental import pallas as pl
from jax.experimental.pallas import tpu as pltpu
from jax.sharding import PartitionSpec as P

BLOCK_WIDTH = 4
BLOCK_CAP = 7
CHUNK = 8
META_DIGITS = 5
AXES = ("group", "blk")
LANES = 128


def meta_digits(cluster, global_index):
    return (
        jnp.ones_like(cluster),
        cluster % BLOCK_WIDTH,
        global_index // 4096,
        (global_index // 64) % 64,
        global_index % 64,
    )


def pack_kernel(x_ref, idx_ref, cols_ref, out_ref):
    x = x_ref[...]
    squares = jnp.sum(x * x, axis=1, keepdims=True)
    unit = (x * lax.rsqrt(squares + 1e-06)).astype(jnp.bfloat16)
    row_count = x_ref.shape[0]
    slots = out_ref.shape[0]
    slot_at = lax.broadcasted_iota(jnp.int32, (slots, row_count), 0)
    picks = (slot_at == idx_ref[0:1, :]).astype(jnp.bfloat16)
    rows = jnp.dot(picks, unit, preferred_element_type=jnp.float32)
    out_ref[...] = rows.astype(jnp.bfloat16)

    cols = cols_ref[...]
    column = lax.broadcasted_iota(jnp.int32, (row_count, LANES), 1)
    spread = jnp.zeros((row_count, LANES), jnp.int32)
    for t in range(META_DIGITS):
        spread = jnp.where(column == t * CHUNK + cols[:, 0:1], cols[:, t + 1 : t + 2], spread)
    meta_picks = (slot_at == idx_ref[1:2, :]).astype(jnp.bfloat16)
    meta = jnp.dot(meta_picks, spread.astype(jnp.bfloat16), preferred_element_type=jnp.float32)
    out_ref[:, :LANES] = (rows[:, :LANES] + meta).astype(jnp.bfloat16)


def pack(embeddings, slot, meta_slot, rank, digits, slots):
    row_count, feat_width = embeddings.shape
    vmem = pltpu.MemorySpace.VMEM
    unused = jnp.zeros_like(slot)
    index_rows = jnp.stack([slot, meta_slot] + [unused] * 6, axis=0)
    cols = jnp.stack([rank, *digits] + [unused] * (7 - len(digits)), axis=1)
    return pl.pallas_call(
        pack_kernel,
        out_shape=jax.ShapeDtypeStruct((slots, feat_width), jnp.bfloat16),
        in_specs=[pl.BlockSpec(memory_space=vmem)] * 3,
        out_specs=pl.BlockSpec(memory_space=vmem),
        compiler_params=pltpu.CompilerParams(vmem_limit_bytes=48 * 1024 * 1024),
    )(embeddings, index_rows, cols)


def score_kernel(got_ref, key_ref, query_ref, best_ref):
    got = got_ref[...]
    cosine = lax.dot_general(
        got, got, (((1,), (1,)), ((), ())), preferred_element_type=jnp.float32
    )
    key = key_ref[...]
    query = query_ref[...]
    usable = (
        (key[:, 0:1] > 0)
        & (key[:, 1:2] == query[1:2, :])
        & (key[:, 2:3] < query[2:3, :])
    )
    best_ref[...] = jnp.max(jnp.where(usable, cosine, jnp.float32(-1.0)), axis=0, keepdims=True)


def score(got_rows, valid, sub, ids):
    slots = got_rows.shape[0]
    vmem = pltpu.MemorySpace.VMEM
    unused = jnp.zeros_like(ids)
    fields = [valid.astype(jnp.int32), sub, ids] + [unused] * 5
    return pl.pallas_call(
        score_kernel,
        out_shape=jax.ShapeDtypeStruct((1, slots), jnp.float32),
        in_specs=[pl.BlockSpec(memory_space=vmem)] * 3,
        out_specs=pl.BlockSpec(memory_space=vmem),
        compiler_params=pltpu.CompilerParams(vmem_limit_bytes=48 * 1024 * 1024),
    )(got_rows, jnp.stack(fields, axis=1), jnp.stack(fields, axis=0))


def on_device(embeddings, cluster, global_index, send_counts):
    row_count, feat_width = embeddings.shape
    blocks = lax.axis_size("blk")
    devices = lax.axis_size("group") * blocks
    slots = devices * CHUNK
    small = lax.optimization_barrier(
        jnp.concatenate([cluster, global_index, send_counts[0]])
    )
    cluster = small[:row_count]
    global_index = small[row_count : 2 * row_count]
    counts = small[2 * row_count :]
    groups = counts.shape[0]
    upto = jnp.arange(groups)[:, None] >= jnp.arange(groups)[None, :]
    cum_ends = jnp.sum(jnp.where(upto, counts[None, :], 0), axis=1)

    position = jnp.arange(row_count, dtype=jnp.int32)
    owner_group = jnp.sum((position[:, None] >= cum_ends[None, :]).astype(jnp.int32), axis=1)
    dest = owner_group * blocks + cluster // BLOCK_WIDTH
    earlier = (dest[:, None] == dest[None, :]) & (position[None, :] < position[:, None])
    rank = jnp.sum(earlier.astype(jnp.int32), axis=1)
    slot = dest * CHUNK + rank

    send = pack(
        embeddings, slot, dest * CHUNK + CHUNK - 1, rank, meta_digits(cluster, global_index), slots
    ).reshape(devices, CHUNK, feat_width)
    slot_ids = jnp.arange(slots, dtype=jnp.int32)
    picks = slot_ids[:, None] == slot[None, :]

    got = lax.all_to_all(send, AXES, 0, 0, tiled=True)
    got_rows = got.reshape(slots, feat_width)
    coded = got[:, CHUNK - 1, : META_DIGITS * CHUNK].astype(jnp.int32)

    def digit(t):
        return coded[:, t * CHUNK : (t + 1) * CHUNK].reshape(slots)

    got_valid = digit(0) > 0
    got_sub = digit(1)
    got_ids = digit(2) * 4096 + digit(3) * 64 + digit(4)

    best = score(got_rows, got_valid, got_sub, got_ids)

    wide = jnp.pad(best.reshape(devices, CHUNK), ((0, 0), (0, LANES - CHUNK)))
    returned = lax.all_to_all(wide, AXES, 0, 0, tiled=True)[:, :CHUNK]
    return jnp.sum(jnp.where(picks, returned.reshape(slots, 1), jnp.float32(0.0)), axis=0)


def solution(mesh):
    placed = (
        P(AXES, None),
        P(AXES),
        P(AXES),
        P(AXES, None),
    )
    return jax.shard_map(
        on_device, mesh=mesh, in_specs=placed, out_specs=P(AXES), check_vma=False
    )
```

```python
import jax
import jax.numpy as jnp
from jax import lax
from jax.experimental import pallas as pl
from jax.experimental.pallas import tpu as pltpu
from jax.sharding import PartitionSpec as P

BLOCK_WIDTH = 4
BLOCK_CAP = 7
CHUNK = 8
META_DIGITS = 5
AXES = ("group", "blk")
LANES = 128
VMEM_LIMIT = 60 * 1024 * 1024


def meta_digits(cluster, global_index):
    return (
        jnp.ones_like(cluster),
        cluster % BLOCK_WIDTH,
        global_index // 4096,
        (global_index // 64) % 64,
        global_index % 64,
    )


def pack_kernel(x_hbm, idx_ref, cols_ref, out_ref, x_buf, unit_buf, sems):
    pieces = sems.shape[0]
    piece = x_buf.shape[0] // pieces
    copies = [
        pltpu.make_async_copy(
            x_hbm.at[pl.ds(j * piece, piece)], x_buf.at[pl.ds(j * piece, piece)], sems.at[j]
        )
        for j in range(pieces)
    ]
    for copy in copies:
        copy.start()
    for j, copy in enumerate(copies):
        copy.wait()
        x = x_buf[pl.ds(j * piece, piece), :]
        squares = jnp.sum(x * x, axis=1, keepdims=True)
        unit_buf[pl.ds(j * piece, piece), :] = (x * lax.rsqrt(squares + 1e-06)).astype(jnp.bfloat16)
    unit = unit_buf[...]
    x_ref = x_buf
    row_count = x_ref.shape[0]
    slots = out_ref.shape[0]
    slot_at = lax.broadcasted_iota(jnp.int32, (slots, row_count), 0)
    picks = (slot_at == idx_ref[0:1, :]).astype(jnp.bfloat16)
    rows = jnp.dot(picks, unit, preferred_element_type=jnp.float32)
    out_ref[...] = rows.astype(jnp.bfloat16)

    cols = cols_ref[...]
    column = lax.broadcasted_iota(jnp.int32, (row_count, LANES), 1)
    spread = jnp.zeros((row_count, LANES), jnp.int32)
    for t in range(META_DIGITS):
        spread = jnp.where(column == t * CHUNK + cols[:, 0:1], cols[:, t + 1 : t + 2], spread)
    meta_picks = (slot_at == idx_ref[1:2, :]).astype(jnp.bfloat16)
    meta = jnp.dot(meta_picks, spread.astype(jnp.bfloat16), preferred_element_type=jnp.float32)
    out_ref[:, :LANES] = (rows[:, :LANES] + meta).astype(jnp.bfloat16)


def pack(embeddings, slot, meta_slot, rank, digits, slots):
    row_count, feat_width = embeddings.shape
    vmem = pltpu.MemorySpace.VMEM
    unused = jnp.zeros_like(slot)
    index_rows = jnp.stack([slot, meta_slot] + [unused] * 6, axis=0)
    cols = jnp.stack([rank, *digits] + [unused] * (7 - len(digits)), axis=1)
    return pl.pallas_call(
        pack_kernel,
        out_shape=jax.ShapeDtypeStruct((slots, feat_width), jnp.bfloat16),
        in_specs=[pl.BlockSpec(memory_space=pl.ANY)] + [pl.BlockSpec(memory_space=vmem)] * 2,
        out_specs=pl.BlockSpec(memory_space=vmem),
        scratch_shapes=[
            pltpu.VMEM((row_count, feat_width), jnp.float32),
            pltpu.VMEM((row_count, feat_width), jnp.bfloat16),
            pltpu.SemaphoreType.DMA((4,)),
        ],
        compiler_params=pltpu.CompilerParams(vmem_limit_bytes=VMEM_LIMIT),
    )(embeddings, index_rows, cols)


def on_device(embeddings, cluster, global_index, send_counts):
    row_count, feat_width = embeddings.shape
    blocks = lax.axis_size("blk")
    devices = lax.axis_size("group") * blocks
    slots = devices * CHUNK
    small = lax.optimization_barrier(
        jnp.concatenate([cluster, global_index, send_counts[0]])
    )
    cluster = small[:row_count]
    global_index = small[row_count : 2 * row_count]
    counts = small[2 * row_count :]
    groups = counts.shape[0]
    upto = jnp.arange(groups)[:, None] >= jnp.arange(groups)[None, :]
    cum_ends = jnp.sum(jnp.where(upto, counts[None, :], 0), axis=1)

    position = jnp.arange(row_count, dtype=jnp.int32)
    owner_group = jnp.sum((position[:, None] >= cum_ends[None, :]).astype(jnp.int32), axis=1)
    dest = owner_group * blocks + cluster // BLOCK_WIDTH
    earlier = (dest[:, None] == dest[None, :]) & (position[None, :] < position[:, None])
    rank = jnp.sum(earlier.astype(jnp.int32), axis=1)
    slot = dest * CHUNK + rank

    send = pack(
        embeddings, slot, dest * CHUNK + CHUNK - 1, rank, meta_digits(cluster, global_index), slots
    ).reshape(devices, CHUNK, feat_width)
    slot_ids = jnp.arange(slots, dtype=jnp.int32)
    picks = slot_ids[:, None] == slot[None, :]

    got = lax.all_to_all(send, AXES, 0, 0, tiled=True)
    got_rows = got.reshape(slots, feat_width)
    coded = got[:, CHUNK - 1, : META_DIGITS * CHUNK].astype(jnp.int32)

    def digit(t):
        return coded[:, t * CHUNK : (t + 1) * CHUNK].reshape(slots)

    got_valid = digit(0) > 0
    got_sub = digit(1)
    got_ids = digit(2) * 4096 + digit(3) * 64 + digit(4)

    cosine = lax.dot_general(
        got_rows, got_rows, (((1,), (1,)), ((), ())), preferred_element_type=jnp.float32
    )
    usable = (
        got_valid[None, :]
        & (got_sub[:, None] == got_sub[None, :])
        & (got_ids[None, :] < got_ids[:, None])
    )
    best = jnp.max(jnp.where(usable, cosine, jnp.float32(-1.0)), axis=1)

    wide = jnp.pad(best.reshape(devices, CHUNK), ((0, 0), (0, LANES - CHUNK)))
    returned = lax.all_to_all(wide, AXES, 0, 0, tiled=True)[:, :CHUNK]
    return jnp.sum(jnp.where(picks, returned.reshape(slots, 1), jnp.float32(0.0)), axis=0)


def solution(mesh):
    placed = (
        P(AXES, None),
        P(AXES),
        P(AXES),
        P(AXES, None),
    )
    return jax.shard_map(
        on_device, mesh=mesh, in_specs=placed, out_specs=P(AXES), check_vma=False
    )
```

```python
import jax
import jax.numpy as jnp
from jax import lax
from jax.experimental import pallas as pl
from jax.experimental.pallas import tpu as pltpu
from jax.sharding import PartitionSpec as P

BLOCK_WIDTH = 4
BLOCK_CAP = 7
CHUNK = 8
META_DIGITS = 5
AXES = ("group", "blk")
LANES = 128
VMEM_LIMIT = 50 * 1024 * 1024


def meta_digits(cluster, global_index):
    return (
        jnp.ones_like(cluster),
        cluster % BLOCK_WIDTH,
        global_index // 4096,
        (global_index // 64) % 64,
        global_index % 64,
    )


def pack_kernel(x_hbm, idx_ref, cols_ref, out_ref, x_buf, unit_buf, sems):
    pieces = sems.shape[0]
    piece = x_buf.shape[0] // pieces
    copies = [
        pltpu.make_async_copy(
            x_hbm.at[pl.ds(j * piece, piece)], x_buf.at[pl.ds(j * piece, piece)], sems.at[j]
        )
        for j in range(pieces)
    ]
    for copy in copies:
        copy.start()
    for j, copy in enumerate(copies):
        copy.wait()
        x = x_buf[pl.ds(j * piece, piece), :]
        squares = jnp.sum(x * x, axis=1, keepdims=True)
        unit_buf[pl.ds(j * piece, piece), :] = (x * lax.rsqrt(squares + 1e-06)).astype(jnp.bfloat16)
    unit = unit_buf[...]
    x_ref = x_buf
    row_count = x_ref.shape[0]
    slots = out_ref.shape[0]
    slot_at = lax.broadcasted_iota(jnp.int32, (slots, row_count), 0)
    picks = (slot_at == idx_ref[0:1, :]).astype(jnp.bfloat16)
    rows = jnp.dot(picks, unit, preferred_element_type=jnp.float32)
    out_ref[...] = rows.astype(jnp.bfloat16)

    cols = cols_ref[...]
    column = lax.broadcasted_iota(jnp.int32, (row_count, LANES), 1)
    spread = jnp.zeros((row_count, LANES), jnp.int32)
    for t in range(META_DIGITS):
        spread = jnp.where(column == t * CHUNK + cols[:, 0:1], cols[:, t + 1 : t + 2], spread)
    meta_picks = (slot_at == idx_ref[1:2, :]).astype(jnp.bfloat16)
    meta = jnp.dot(meta_picks, spread.astype(jnp.bfloat16), preferred_element_type=jnp.float32)
    out_ref[:, :LANES] = (rows[:, :LANES] + meta).astype(jnp.bfloat16)


def pack(embeddings, slot, meta_slot, rank, digits, slots):
    row_count, feat_width = embeddings.shape
    vmem = pltpu.MemorySpace.VMEM
    unused = jnp.zeros_like(slot)
    index_rows = jnp.stack([slot, meta_slot] + [unused] * 6, axis=0)
    cols = jnp.stack([rank, *digits] + [unused] * (7 - len(digits)), axis=1)
    return pl.pallas_call(
        pack_kernel,
        out_shape=jax.ShapeDtypeStruct((slots, feat_width), jnp.bfloat16),
        in_specs=[pl.BlockSpec(memory_space=pl.ANY)] + [pl.BlockSpec(memory_space=vmem)] * 2,
        out_specs=pl.BlockSpec(memory_space=vmem),
        scratch_shapes=[
            pltpu.VMEM((row_count, feat_width), jnp.float32),
            pltpu.VMEM((row_count, feat_width), jnp.bfloat16),
            pltpu.SemaphoreType.DMA((4,)),
        ],
        compiler_params=pltpu.CompilerParams(vmem_limit_bytes=VMEM_LIMIT),
    )(embeddings, index_rows, cols)


def on_device(embeddings, cluster, global_index, send_counts):
    row_count, feat_width = embeddings.shape
    blocks = lax.axis_size("blk")
    devices = lax.axis_size("group") * blocks
    slots = devices * CHUNK
    small = lax.optimization_barrier(
        jnp.concatenate([cluster, global_index, send_counts[0]])
    )
    cluster = small[:row_count]
    global_index = small[row_count : 2 * row_count]
    counts = small[2 * row_count :]
    groups = counts.shape[0]
    upto = jnp.arange(groups)[:, None] >= jnp.arange(groups)[None, :]
    cum_ends = jnp.sum(jnp.where(upto, counts[None, :], 0), axis=1)

    position = jnp.arange(row_count, dtype=jnp.int32)
    owner_group = jnp.sum((position[:, None] >= cum_ends[None, :]).astype(jnp.int32), axis=1)
    dest = owner_group * blocks + cluster // BLOCK_WIDTH
    earlier = (dest[:, None] == dest[None, :]) & (position[None, :] < position[:, None])
    rank = jnp.sum(earlier.astype(jnp.int32), axis=1)
    slot = dest * CHUNK + rank

    send = pack(
        embeddings, slot, dest * CHUNK + CHUNK - 1, rank, meta_digits(cluster, global_index), slots
    ).reshape(devices, CHUNK, feat_width)
    slot_ids = jnp.arange(slots, dtype=jnp.int32)
    picks = slot_ids[:, None] == slot[None, :]

    got = lax.all_to_all(send, AXES, 0, 0, tiled=True)
    got_rows = got.reshape(slots, feat_width)
    coded = got[:, CHUNK - 1, : META_DIGITS * CHUNK].astype(jnp.int32)

    def digit(t):
        return coded[:, t * CHUNK : (t + 1) * CHUNK].reshape(slots)

    got_valid = digit(0) > 0
    got_sub = digit(1)
    got_ids = digit(2) * 4096 + digit(3) * 64 + digit(4)

    cosine = lax.dot_general(
        got_rows, got_rows, (((1,), (1,)), ((), ())), preferred_element_type=jnp.float32
    )
    usable = (
        got_valid[None, :]
        & (got_sub[:, None] == got_sub[None, :])
        & (got_ids[None, :] < got_ids[:, None])
    )
    best = jnp.max(jnp.where(usable, cosine, jnp.float32(-1.0)), axis=1)

    wide = jnp.pad(best.reshape(devices, CHUNK), ((0, 0), (0, LANES - CHUNK)))
    returned = lax.all_to_all(wide, AXES, 0, 0, tiled=True)[:, :CHUNK]
    return jnp.sum(jnp.where(picks, returned.reshape(slots, 1), jnp.float32(0.0)), axis=0)


def solution(mesh):
    placed = (
        P(AXES, None),
        P(AXES),
        P(AXES),
        P(AXES, None),
    )
    return jax.shard_map(
        on_device, mesh=mesh, in_specs=placed, out_specs=P(AXES), check_vma=False
    )
```

```python
import jax
import jax.numpy as jnp
from jax import lax
from jax.experimental import pallas as pl
from jax.experimental.pallas import tpu as pltpu
from jax.sharding import PartitionSpec as P

BLOCK_WIDTH = 4
BLOCK_CAP = 7
CHUNK = 8
META_DIGITS = 5
AXES = ("group", "blk")
LANES = 128
VMEM_LIMIT = 50 * 1024 * 1024


def meta_digits(cluster, global_index):
    return (
        jnp.ones_like(cluster),
        cluster % BLOCK_WIDTH,
        global_index // 4096,
        (global_index // 64) % 64,
        global_index % 64,
    )


def pack_kernel(x_hbm, idx_ref, cols_ref, out_ref, x_buf, sems):
    row_count = x_buf.shape[0]
    slots = out_ref.shape[0]
    starts = list(range(0, row_count - LANES, LANES))
    ends = starts[1:] + [row_count]
    copies = [
        pltpu.make_async_copy(
            x_hbm.at[pl.ds(lo, hi - lo)], x_buf.at[pl.ds(lo, hi - lo)], sems.at[j]
        )
        for j, (lo, hi) in enumerate(zip(starts, ends))
    ]
    for copy in copies:
        copy.start()

    cols = cols_ref[...]
    column = lax.broadcasted_iota(jnp.int32, (row_count, LANES), 1)
    spread = jnp.zeros((row_count, LANES), jnp.int32)
    for t in range(META_DIGITS):
        spread = jnp.where(column == t * CHUNK + cols[:, 0:1], cols[:, t + 1 : t + 2], spread)
    meta_at = lax.broadcasted_iota(jnp.int32, (slots, row_count), 0)
    meta_picks = (meta_at == idx_ref[1:2, :]).astype(jnp.bfloat16)
    meta = jnp.dot(meta_picks, spread.astype(jnp.bfloat16), preferred_element_type=jnp.float32)

    rows = None
    for (lo, hi), copy in zip(zip(starts, ends), copies):
        copy.wait()
        x = x_buf[pl.ds(lo, hi - lo), :]
        squares = jnp.sum(x * x, axis=1, keepdims=True)
        unit = (x * lax.rsqrt(squares + 1e-06)).astype(jnp.bfloat16)
        slot_at = lax.broadcasted_iota(jnp.int32, (slots, hi - lo), 0)
        picks = (slot_at == idx_ref[0:1, lo:hi]).astype(jnp.bfloat16)
        part = jnp.dot(picks, unit, preferred_element_type=jnp.float32)
        rows = part if rows is None else rows + part
    out_ref[...] = rows.astype(jnp.bfloat16)
    out_ref[:, :LANES] = (rows[:, :LANES] + meta).astype(jnp.bfloat16)


def pack(embeddings, slot, meta_slot, rank, digits, slots):
    row_count, feat_width = embeddings.shape
    vmem = pltpu.MemorySpace.VMEM
    unused = jnp.zeros_like(slot)
    index_rows = jnp.stack([slot, meta_slot] + [unused] * 6, axis=0)
    cols = jnp.stack([rank, *digits] + [unused] * (7 - len(digits)), axis=1)
    return pl.pallas_call(
        pack_kernel,
        out_shape=jax.ShapeDtypeStruct((slots, feat_width), jnp.bfloat16),
        in_specs=[pl.BlockSpec(memory_space=pl.ANY)] + [pl.BlockSpec(memory_space=vmem)] * 2,
        out_specs=pl.BlockSpec(memory_space=vmem),
        scratch_shapes=[
            pltpu.VMEM((row_count, feat_width), jnp.float32),
            pltpu.SemaphoreType.DMA((row_count // LANES,)),
        ],
        compiler_params=pltpu.CompilerParams(vmem_limit_bytes=VMEM_LIMIT),
    )(embeddings, index_rows, cols)


def on_device(embeddings, cluster, global_index, send_counts):
    row_count, feat_width = embeddings.shape
    blocks = lax.axis_size("blk")
    devices = lax.axis_size("group") * blocks
    slots = devices * CHUNK
    small = lax.optimization_barrier(
        jnp.concatenate([cluster, global_index, send_counts[0]])
    )
    cluster = small[:row_count]
    global_index = small[row_count : 2 * row_count]
    counts = small[2 * row_count :]
    groups = counts.shape[0]
    upto = jnp.arange(groups)[:, None] >= jnp.arange(groups)[None, :]
    cum_ends = jnp.sum(jnp.where(upto, counts[None, :], 0), axis=1)

    position = jnp.arange(row_count, dtype=jnp.int32)
    owner_group = jnp.sum((position[:, None] >= cum_ends[None, :]).astype(jnp.int32), axis=1)
    dest = owner_group * blocks + cluster // BLOCK_WIDTH
    earlier = (dest[:, None] == dest[None, :]) & (position[None, :] < position[:, None])
    rank = jnp.sum(earlier.astype(jnp.int32), axis=1)
    slot = dest * CHUNK + rank

    send = pack(
        embeddings, slot, dest * CHUNK + CHUNK - 1, rank, meta_digits(cluster, global_index), slots
    ).reshape(devices, CHUNK, feat_width)
    slot_ids = jnp.arange(slots, dtype=jnp.int32)
    picks = slot_ids[:, None] == slot[None, :]

    got = lax.all_to_all(send, AXES, 0, 0, tiled=True)
    got_rows = got.reshape(slots, feat_width)
    coded = got[:, CHUNK - 1, : META_DIGITS * CHUNK].astype(jnp.int32)

    def digit(t):
        return coded[:, t * CHUNK : (t + 1) * CHUNK].reshape(slots)

    got_valid = digit(0) > 0
    got_sub = digit(1)
    got_ids = digit(2) * 4096 + digit(3) * 64 + digit(4)

    cosine = lax.dot_general(
        got_rows, got_rows, (((1,), (1,)), ((), ())), preferred_element_type=jnp.float32
    )
    usable = (
        got_valid[None, :]
        & (got_sub[:, None] == got_sub[None, :])
        & (got_ids[None, :] < got_ids[:, None])
    )
    best = jnp.max(jnp.where(usable, cosine, jnp.float32(-1.0)), axis=1)

    wide = jnp.pad(best.reshape(devices, CHUNK), ((0, 0), (0, LANES - CHUNK)))
    returned = lax.all_to_all(wide, AXES, 0, 0, tiled=True)[:, :CHUNK]
    return jnp.sum(jnp.where(picks, returned.reshape(slots, 1), jnp.float32(0.0)), axis=0)


def solution(mesh):
    placed = (
        P(AXES, None),
        P(AXES),
        P(AXES),
        P(AXES, None),
    )
    return jax.shard_map(
        on_device, mesh=mesh, in_specs=placed, out_specs=P(AXES), check_vma=False
    )
```

```python
import functools

import jax
import jax.numpy as jnp
from jax import lax
from jax.experimental import pallas as pl
from jax.experimental.pallas import tpu as pltpu
from jax.sharding import PartitionSpec as P

BLOCK_WIDTH = 4
BLOCK_CAP = 7
CHUNK = 8
META_DIGITS = 5
AXES = ("group", "blk")
LANES = 128
VMEM_LIMIT = 50 * 1024 * 1024


def pack_kernel(blocks, x_hbm, small_ref, out_ref, slot_ref, x_buf, unit_buf, sems):
    pieces = sems.shape[0]
    row_count = x_buf.shape[0]
    piece = row_count // pieces
    slots = out_ref.shape[0]
    copies = [
        pltpu.make_async_copy(
            x_hbm.at[pl.ds(j * piece, piece)], x_buf.at[pl.ds(j * piece, piece)], sems.at[j]
        )
        for j in range(pieces)
    ]
    for copy in copies:
        copy.start()

    pos_row = lax.broadcasted_iota(jnp.int32, (1, row_count), 1)
    pos_col = lax.broadcasted_iota(jnp.int32, (row_count, 1), 0)
    cl_row = small_ref[0:1, :]
    gi_row = small_ref[1:2, :]
    counts_row = small_ref[2:3, :]
    owner_row = jnp.zeros((1, row_count), jnp.int32)
    for g in range(blocks.groups):
        end = jnp.sum(jnp.where(pos_row <= g, counts_row, 0), axis=1, keepdims=True)
        owner_row = owner_row + (pos_row >= end).astype(jnp.int32)
    dest_row = owner_row * blocks.blocks + lax.shift_right_logical(cl_row, 2)
    on_diag = pos_col == pos_row
    dest_col = jnp.sum(jnp.where(on_diag, dest_row, 0), axis=1, keepdims=True)
    cl_col = jnp.sum(jnp.where(on_diag, cl_row, 0), axis=1, keepdims=True)
    gi_col = jnp.sum(jnp.where(on_diag, gi_row, 0), axis=1, keepdims=True)
    same = dest_col == dest_row
    rank_row = jnp.sum((same & (pos_col < pos_row)).astype(jnp.int32), axis=0, keepdims=True)
    rank_col = jnp.sum((same & (pos_row < pos_col)).astype(jnp.int32), axis=1, keepdims=True)
    slot_row = dest_row * CHUNK + rank_row
    slot_ref[...] = slot_row

    digits = (
        jnp.ones_like(cl_col),
        cl_col & (BLOCK_WIDTH - 1),
        lax.shift_right_logical(gi_col, 12),
        lax.shift_right_logical(gi_col, 6) & 63,
        gi_col & 63,
    )
    column = lax.broadcasted_iota(jnp.int32, (row_count, LANES), 1)
    spread = jnp.zeros((row_count, LANES), jnp.int32)
    for t, digit in enumerate(digits):
        spread = jnp.where(column == t * CHUNK + rank_col, digit, spread)
    slot_at = lax.broadcasted_iota(jnp.int32, (slots, row_count), 0)
    meta_picks = (slot_at == dest_row * CHUNK + CHUNK - 1).astype(jnp.bfloat16)
    meta = jnp.dot(meta_picks, spread.astype(jnp.bfloat16), preferred_element_type=jnp.float32)
    picks = (slot_at == slot_row).astype(jnp.bfloat16)

    for j, copy in enumerate(copies):
        copy.wait()
        x = x_buf[pl.ds(j * piece, piece), :]
        squares = jnp.sum(x * x, axis=1, keepdims=True)
        unit_buf[pl.ds(j * piece, piece), :] = (x * lax.rsqrt(squares + 1e-06)).astype(jnp.bfloat16)
    rows = jnp.dot(picks, unit_buf[...], preferred_element_type=jnp.float32)
    out_ref[...] = rows.astype(jnp.bfloat16)
    out_ref[:, :LANES] = (rows[:, :LANES] + meta).astype(jnp.bfloat16)


class MeshSizes:
    def __init__(self, groups, blocks):
        self.groups = groups
        self.blocks = blocks


def pack(embeddings, cluster, global_index, counts, sizes, slots):
    row_count, feat_width = embeddings.shape
    vmem = pltpu.MemorySpace.VMEM
    joined = lax.optimization_barrier(jnp.concatenate([cluster, global_index, counts]))
    small = jnp.stack(
        [
            joined[:row_count],
            joined[row_count : 2 * row_count],
            jnp.pad(joined[2 * row_count :], (0, row_count - counts.shape[0])),
        ],
        axis=0,
    )
    return pl.pallas_call(
        functools.partial(pack_kernel, sizes),
        out_shape=(
            jax.ShapeDtypeStruct((slots, feat_width), jnp.bfloat16),
            jax.ShapeDtypeStruct((1, row_count), jnp.int32),
        ),
        in_specs=[pl.BlockSpec(memory_space=pl.ANY), pl.BlockSpec(memory_space=vmem)],
        out_specs=(pl.BlockSpec(memory_space=vmem), pl.BlockSpec(memory_space=vmem)),
        scratch_shapes=[
            pltpu.VMEM((row_count, feat_width), jnp.float32),
            pltpu.VMEM((row_count, feat_width), jnp.bfloat16),
            pltpu.SemaphoreType.DMA((4,)),
        ],
        compiler_params=pltpu.CompilerParams(vmem_limit_bytes=VMEM_LIMIT),
    )(embeddings, small)


def on_device(embeddings, cluster, global_index, send_counts):
    row_count, feat_width = embeddings.shape
    blocks = lax.axis_size("blk")
    devices = lax.axis_size("group") * blocks
    slots = devices * CHUNK
    sizes = MeshSizes(lax.axis_size("group"), blocks)
    send, slot = pack(embeddings, cluster, global_index, send_counts[0], sizes, slots)
    send = send.reshape(devices, CHUNK, feat_width)
    slot_ids = jnp.arange(slots, dtype=jnp.int32)
    picks = slot_ids[:, None] == slot

    got = lax.all_to_all(send, AXES, 0, 0, tiled=True)
    got_rows = got.reshape(slots, feat_width)
    coded = got[:, CHUNK - 1, : META_DIGITS * CHUNK].astype(jnp.int32)

    def digit(t):
        return coded[:, t * CHUNK : (t + 1) * CHUNK].reshape(slots)

    got_valid = digit(0) > 0
    got_sub = digit(1)
    got_ids = digit(2) * 4096 + digit(3) * 64 + digit(4)

    cosine = lax.dot_general(
        got_rows, got_rows, (((1,), (1,)), ((), ())), preferred_element_type=jnp.float32
    )
    usable = (
        got_valid[None, :]
        & (got_sub[:, None] == got_sub[None, :])
        & (got_ids[None, :] < got_ids[:, None])
    )
    best = jnp.max(jnp.where(usable, cosine, jnp.float32(-1.0)), axis=1)

    wide = jnp.pad(best.reshape(devices, CHUNK), ((0, 0), (0, LANES - CHUNK)))
    returned = lax.all_to_all(wide, AXES, 0, 0, tiled=True)[:, :CHUNK]
    return jnp.sum(jnp.where(picks, returned.reshape(slots, 1), jnp.float32(0.0)), axis=0)


def solution(mesh):
    placed = (
        P(AXES, None),
        P(AXES),
        P(AXES),
        P(AXES, None),
    )
    return jax.shard_map(
        on_device, mesh=mesh, in_specs=placed, out_specs=P(AXES), check_vma=False
    )
```

```python
import functools

import jax
import jax.numpy as jnp
from jax import lax
from jax.experimental import pallas as pl
from jax.experimental.pallas import tpu as pltpu
from jax.sharding import PartitionSpec as P

BLOCK_WIDTH = 4
BLOCK_CAP = 7
CHUNK = 8
META_DIGITS = 5
AXES = ("group", "blk")
LANES = 128
VMEM_LIMIT = 50 * 1024 * 1024


def pack_kernel(blocks, x_hbm, small_ref, out_ref, slot_ref, x_buf, unit_buf, sems):
    pieces = sems.shape[0]
    row_count = x_buf.shape[0]
    piece = row_count // pieces
    slots = out_ref.shape[0]
    copies = [
        pltpu.make_async_copy(
            x_hbm.at[pl.ds(j * piece, piece)], x_buf.at[pl.ds(j * piece, piece)], sems.at[j]
        )
        for j in range(pieces)
    ]
    for copy in copies:
        copy.start()

    pos_row = lax.broadcasted_iota(jnp.int32, (1, row_count), 1)
    pos_col = lax.broadcasted_iota(jnp.int32, (row_count, 1), 0)
    cl_row = small_ref[0:1, :]
    gi_row = small_ref[1:2, :]
    counts_row = small_ref[2:3, :]
    owner_row = jnp.zeros((1, row_count), jnp.int32)
    for g in range(blocks.groups):
        end = jnp.sum(jnp.where(pos_row <= g, counts_row, 0), axis=1, keepdims=True)
        owner_row = owner_row + (pos_row >= end).astype(jnp.int32)
    dest_row = owner_row * blocks.blocks + lax.shift_right_logical(cl_row, 2)
    devices = slots // CHUNK
    dest_hot = lax.broadcasted_iota(jnp.int32, (devices, row_count), 0) == dest_row
    before = pos_col < pos_row
    counted = jnp.dot(
        dest_hot.astype(jnp.bfloat16), before.astype(jnp.bfloat16), preferred_element_type=jnp.float32
    )
    rank_row = jnp.sum(jnp.where(dest_hot, counted, 0.0), axis=0, keepdims=True).astype(jnp.int32)
    slot_row = dest_row * CHUNK + rank_row
    slot_ref[...] = slot_row

    digits = (
        jnp.ones_like(cl_row),
        cl_row & (BLOCK_WIDTH - 1),
        lax.shift_right_logical(gi_row, 12),
        lax.shift_right_logical(gi_row, 6) & 63,
        gi_row & 63,
    )
    column = lax.broadcasted_iota(jnp.int32, (LANES, row_count), 0)
    spread = jnp.zeros((LANES, row_count), jnp.int32)
    for t, digit in enumerate(digits):
        spread = jnp.where(column == t * CHUNK + rank_row, digit, spread)
    slot_at = lax.broadcasted_iota(jnp.int32, (slots, row_count), 0)
    meta_picks = (slot_at == dest_row * CHUNK + CHUNK - 1).astype(jnp.bfloat16)
    meta = lax.dot_general(
        meta_picks,
        spread.astype(jnp.bfloat16),
        (((1,), (1,)), ((), ())),
        preferred_element_type=jnp.float32,
    )
    picks = (slot_at == slot_row).astype(jnp.bfloat16)

    for j, copy in enumerate(copies):
        copy.wait()
        x = x_buf[pl.ds(j * piece, piece), :]
        squares = jnp.sum(x * x, axis=1, keepdims=True)
        unit_buf[pl.ds(j * piece, piece), :] = (x * lax.rsqrt(squares + 1e-06)).astype(jnp.bfloat16)
    rows = jnp.dot(picks, unit_buf[...], preferred_element_type=jnp.float32)
    out_ref[...] = rows.astype(jnp.bfloat16)
    out_ref[:, :LANES] = (rows[:, :LANES] + meta).astype(jnp.bfloat16)


class MeshSizes:
    def __init__(self, groups, blocks):
        self.groups = groups
        self.blocks = blocks


def pack(embeddings, cluster, global_index, counts, sizes, slots):
    row_count, feat_width = embeddings.shape
    vmem = pltpu.MemorySpace.VMEM
    joined = lax.optimization_barrier(jnp.concatenate([cluster, global_index, counts]))
    small = jnp.stack(
        [
            joined[:row_count],
            joined[row_count : 2 * row_count],
            jnp.pad(joined[2 * row_count :], (0, row_count - counts.shape[0])),
        ],
        axis=0,
    )
    return pl.pallas_call(
        functools.partial(pack_kernel, sizes),
        out_shape=(
            jax.ShapeDtypeStruct((slots, feat_width), jnp.bfloat16),
            jax.ShapeDtypeStruct((1, row_count), jnp.int32),
        ),
        in_specs=[pl.BlockSpec(memory_space=pl.ANY), pl.BlockSpec(memory_space=vmem)],
        out_specs=(pl.BlockSpec(memory_space=vmem), pl.BlockSpec(memory_space=vmem)),
        scratch_shapes=[
            pltpu.VMEM((row_count, feat_width), jnp.float32),
            pltpu.VMEM((row_count, feat_width), jnp.bfloat16),
            pltpu.SemaphoreType.DMA((4,)),
        ],
        compiler_params=pltpu.CompilerParams(vmem_limit_bytes=VMEM_LIMIT),
    )(embeddings, small)


def on_device(embeddings, cluster, global_index, send_counts):
    row_count, feat_width = embeddings.shape
    blocks = lax.axis_size("blk")
    devices = lax.axis_size("group") * blocks
    slots = devices * CHUNK
    sizes = MeshSizes(lax.axis_size("group"), blocks)
    send, slot = pack(embeddings, cluster, global_index, send_counts[0], sizes, slots)
    send = send.reshape(devices, CHUNK, feat_width)
    slot_ids = jnp.arange(slots, dtype=jnp.int32)
    picks = slot_ids[:, None] == slot

    got = lax.all_to_all(send, AXES, 0, 0, tiled=True)
    got_rows = got.reshape(slots, feat_width)
    coded = got[:, CHUNK - 1, : META_DIGITS * CHUNK].astype(jnp.int32)

    def digit(t):
        return coded[:, t * CHUNK : (t + 1) * CHUNK].reshape(slots)

    got_valid = digit(0) > 0
    got_sub = digit(1)
    got_ids = digit(2) * 4096 + digit(3) * 64 + digit(4)

    cosine = lax.dot_general(
        got_rows, got_rows, (((1,), (1,)), ((), ())), preferred_element_type=jnp.float32
    )
    usable = (
        got_valid[None, :]
        & (got_sub[:, None] == got_sub[None, :])
        & (got_ids[None, :] < got_ids[:, None])
    )
    best = jnp.max(jnp.where(usable, cosine, jnp.float32(-1.0)), axis=1)

    wide = jnp.pad(best.reshape(devices, CHUNK), ((0, 0), (0, LANES - CHUNK)))
    returned = lax.all_to_all(wide, AXES, 0, 0, tiled=True)[:, :CHUNK]
    return jnp.sum(jnp.where(picks, returned.reshape(slots, 1), jnp.float32(0.0)), axis=0)


def solution(mesh):
    placed = (
        P(AXES, None),
        P(AXES),
        P(AXES),
        P(AXES, None),
    )
    return jax.shard_map(
        on_device, mesh=mesh, in_specs=placed, out_specs=P(AXES), check_vma=False
    )
```

```python
import jax
import jax.numpy as jnp
from jax import lax
from jax.experimental import pallas as pl
from jax.experimental.pallas import tpu as pltpu
from jax.sharding import PartitionSpec as P

BLOCK_WIDTH = 4
BLOCK_CAP = 7
CHUNK = 8
META_DIGITS = 5
AXES = ("group", "blk")
LANES = 128


def meta_digits(cluster, global_index):
    return (
        jnp.ones_like(cluster),
        cluster % BLOCK_WIDTH,
        global_index // 4096,
        (global_index // 64) % 64,
        global_index % 64,
    )


def pack_kernel(x_ref, idx_ref, cols_ref, out_ref):
    x = x_ref[...]
    squares = jnp.sum(x * x, axis=1, keepdims=True)
    unit = (x * lax.rsqrt(squares + 1e-06)).astype(jnp.bfloat16)
    row_count = x_ref.shape[0]
    slots = out_ref.shape[0]
    slot_at = lax.broadcasted_iota(jnp.int32, (slots, row_count), 0)
    picks = (slot_at == idx_ref[0:1, :]).astype(jnp.bfloat16)
    rows = jnp.dot(picks, unit, preferred_element_type=jnp.float32)
    out_ref[...] = rows.astype(jnp.bfloat16)

    cols = cols_ref[...]
    column = lax.broadcasted_iota(jnp.int32, (row_count, LANES), 1)
    spread = jnp.zeros((row_count, LANES), jnp.int32)
    for t in range(META_DIGITS):
        spread = jnp.where(column == t * CHUNK + cols[:, 0:1], cols[:, t + 1 : t + 2], spread)
    meta_picks = (slot_at == idx_ref[1:2, :]).astype(jnp.bfloat16)
    meta = jnp.dot(meta_picks, spread.astype(jnp.bfloat16), preferred_element_type=jnp.float32)
    out_ref[:, :LANES] = (rows[:, :LANES] + meta).astype(jnp.bfloat16)


def pack(embeddings, slot, meta_slot, rank, digits, slots):
    row_count, feat_width = embeddings.shape
    vmem = pltpu.MemorySpace.VMEM
    unused = jnp.zeros_like(slot)
    index_rows = jnp.stack([slot, meta_slot] + [unused] * 6, axis=0)
    cols = jnp.stack([rank, *digits] + [unused] * (7 - len(digits)), axis=1)
    return pl.pallas_call(
        pack_kernel,
        out_shape=jax.ShapeDtypeStruct((slots, feat_width), jnp.bfloat16),
        in_specs=[pl.BlockSpec(memory_space=vmem)] * 3,
        out_specs=pl.BlockSpec(memory_space=vmem),
        compiler_params=pltpu.CompilerParams(vmem_limit_bytes=48 * 1024 * 1024),
    )(embeddings, index_rows, cols)


def on_device(embeddings, cluster, global_index, send_counts):
    row_count, feat_width = embeddings.shape
    blocks = lax.axis_size("blk")
    devices = lax.axis_size("group") * blocks
    slots = devices * CHUNK
    small = lax.optimization_barrier(
        jnp.concatenate([cluster, global_index, send_counts[0]])
    )
    cluster = small[:row_count]
    global_index = small[row_count : 2 * row_count]
    counts = small[2 * row_count :]
    groups = counts.shape[0]
    upto = jnp.arange(groups)[:, None] >= jnp.arange(groups)[None, :]
    cum_ends = jnp.sum(jnp.where(upto, counts[None, :], 0), axis=1)

    position = jnp.arange(row_count, dtype=jnp.int32)
    owner_group = jnp.sum((position[:, None] >= cum_ends[None, :]).astype(jnp.int32), axis=1)
    dest = owner_group * blocks + cluster // BLOCK_WIDTH
    earlier = (dest[:, None] == dest[None, :]) & (position[None, :] < position[:, None])
    rank = jnp.sum(earlier.astype(jnp.int32), axis=1)
    slot = dest * CHUNK + rank

    send = pack(
        embeddings, slot, dest * CHUNK + CHUNK - 1, rank, meta_digits(cluster, global_index), slots
    ).reshape(devices, CHUNK, feat_width)
    slot_ids = jnp.arange(slots, dtype=jnp.int32)
    picks = slot_ids[:, None] == slot[None, :]

    got = lax.all_to_all(send, AXES, 0, 0, tiled=True)
    got_rows = got.reshape(slots, feat_width)
    coded = got[:, CHUNK - 1, : META_DIGITS * CHUNK].astype(jnp.int32)

    def digit(t):
        return coded[:, t * CHUNK : (t + 1) * CHUNK].reshape(slots)

    got_valid = digit(0) > 0
    got_sub = digit(1)
    got_ids = digit(2) * 4096 + digit(3) * 64 + digit(4)

    cosine = lax.dot_general(
        got_rows, got_rows, (((1,), (1,)), ((), ())), preferred_element_type=jnp.float32
    )
    usable = (
        got_valid[:, None]
        & (got_sub[:, None] == got_sub[None, :])
        & (got_ids[:, None] < got_ids[None, :])
    )
    best = jnp.max(jnp.where(usable, cosine, jnp.float32(-1.0)), axis=0)

    wide = jnp.pad(best.reshape(devices, CHUNK), ((0, 0), (0, LANES - CHUNK)))
    returned = lax.all_to_all(wide, AXES, 0, 0, tiled=True)[:, :CHUNK]
    return jnp.sum(jnp.where(picks, returned.reshape(slots, 1), jnp.float32(0.0)), axis=0)


def solution(mesh):
    placed = (
        P(AXES, None),
        P(AXES),
        P(AXES),
        P(AXES, None),
    )
    return jax.shard_map(
        on_device, mesh=mesh, in_specs=placed, out_specs=P(AXES), check_vma=False
    )
```

```python
import jax
import jax.numpy as jnp
from jax import lax
from jax.experimental import pallas as pl
from jax.experimental.pallas import tpu as pltpu
from jax.sharding import PartitionSpec as P

BLOCK_WIDTH = 4
BLOCK_CAP = 7
CHUNK = 8
META_DIGITS = 5
AXES = ("group", "blk")
LANES = 128


def meta_digits(cluster, global_index):
    return (
        jnp.ones_like(cluster),
        cluster % BLOCK_WIDTH,
        global_index // 4096,
        (global_index // 64) % 64,
        global_index % 64,
    )


def pack_kernel(x_ref, idx_ref, cols_ref, out_ref):
    x = x_ref[...]
    squares = jnp.sum(x * x, axis=1, keepdims=True)
    unit = (x * lax.rsqrt(squares + 1e-06)).astype(jnp.bfloat16)
    row_count = x_ref.shape[0]
    slots = out_ref.shape[0]
    slot_at = lax.broadcasted_iota(jnp.int32, (slots, row_count), 0)
    picks = (slot_at == idx_ref[0:1, :]).astype(jnp.bfloat16)
    rows = jnp.dot(picks, unit, preferred_element_type=jnp.float32)
    out_ref[...] = rows.astype(jnp.bfloat16)

    cols = cols_ref[...]
    column = lax.broadcasted_iota(jnp.int32, (row_count, LANES), 1)
    spread = jnp.zeros((row_count, LANES), jnp.int32)
    for t in range(META_DIGITS):
        spread = jnp.where(column == t * CHUNK + cols[:, 0:1], cols[:, t + 1 : t + 2], spread)
    meta_picks = (slot_at == idx_ref[1:2, :]).astype(jnp.bfloat16)
    meta = jnp.dot(meta_picks, spread.astype(jnp.bfloat16), preferred_element_type=jnp.float32)
    out_ref[:, :LANES] = (rows[:, :LANES] + meta).astype(jnp.bfloat16)


def pack(embeddings, slot, meta_slot, rank, digits, slots):
    row_count, feat_width = embeddings.shape
    vmem = pltpu.MemorySpace.VMEM
    unused = jnp.zeros_like(slot)
    index_rows = jnp.stack([slot, meta_slot] + [unused] * 6, axis=0)
    cols = jnp.stack([rank, *digits] + [unused] * (7 - len(digits)), axis=1)
    return pl.pallas_call(
        pack_kernel,
        out_shape=jax.ShapeDtypeStruct((slots, feat_width), jnp.bfloat16),
        in_specs=[pl.BlockSpec(memory_space=vmem)] * 3,
        out_specs=pl.BlockSpec(memory_space=vmem),
        compiler_params=pltpu.CompilerParams(vmem_limit_bytes=48 * 1024 * 1024),
    )(embeddings, index_rows, cols)


def on_device(embeddings, cluster, global_index, send_counts):
    row_count, feat_width = embeddings.shape
    blocks = lax.axis_size("blk")
    devices = lax.axis_size("group") * blocks
    slots = devices * CHUNK
    small = lax.optimization_barrier(
        jnp.concatenate([cluster, global_index, send_counts[0]])
    )
    cluster = small[:row_count]
    global_index = small[row_count : 2 * row_count]
    counts = small[2 * row_count :]
    groups = counts.shape[0]
    upto = jnp.arange(groups)[:, None] >= jnp.arange(groups)[None, :]
    cum_ends = jnp.sum(jnp.where(upto, counts[None, :], 0), axis=1)

    position = jnp.arange(row_count, dtype=jnp.int32)
    owner_group = jnp.sum((position[:, None] >= cum_ends[None, :]).astype(jnp.int32), axis=1)
    dest = owner_group * blocks + cluster // BLOCK_WIDTH
    earlier = (dest[:, None] == dest[None, :]) & (position[None, :] < position[:, None])
    rank = jnp.sum(earlier.astype(jnp.int32), axis=1)
    slot = dest * CHUNK + rank

    send = pack(
        embeddings, slot, dest * CHUNK + CHUNK - 1, rank, meta_digits(cluster, global_index), slots
    ).reshape(devices, CHUNK, feat_width)
    slot_ids = jnp.arange(slots, dtype=jnp.int32)
    picks = slot_ids[:, None] == slot[None, :]

    got = lax.all_to_all(send, AXES, 0, 0, tiled=True)
    got_rows = got.reshape(slots, feat_width)
    coded = got[:, CHUNK - 1, : META_DIGITS * CHUNK].astype(jnp.int32)

    def digit(t):
        return coded[:, t * CHUNK : (t + 1) * CHUNK].reshape(slots)

    got_valid = digit(0) > 0
    got_sub = digit(1)
    got_ids = digit(2) * 4096 + digit(3) * 64 + digit(4)

    cosine = lax.dot_general(
        got_rows, got_rows, (((1,), (1,)), ((), ())), preferred_element_type=jnp.float32
    )
    usable = (
        got_valid[None, :]
        & (got_sub[:, None] == got_sub[None, :])
        & (got_ids[None, :] < got_ids[:, None])
    )
    best = jnp.max(jnp.where(usable, cosine, jnp.float32(-1.0)), axis=1)

    wide = jnp.pad(best.reshape(devices, CHUNK), ((0, 0), (0, LANES - CHUNK)))
    returned = lax.all_to_all(wide, AXES, 0, 0, tiled=True)[:, :CHUNK]
    return jnp.dot(
        returned.reshape(1, slots),
        picks.astype(jnp.float32),
        precision=lax.Precision.HIGHEST,
        preferred_element_type=jnp.float32,
    ).reshape(row_count)


def solution(mesh):
    placed = (
        P(AXES, None),
        P(AXES),
        P(AXES),
        P(AXES, None),
    )
    return jax.shard_map(
        on_device, mesh=mesh, in_specs=placed, out_specs=P(AXES), check_vma=False
    )
```

```python
import jax
import jax.numpy as jnp
from jax import lax
from jax.experimental import pallas as pl
from jax.experimental.pallas import tpu as pltpu
from jax.sharding import PartitionSpec as P

BLOCK_WIDTH = 4
BLOCK_CAP = 7
CHUNK = 8
META_DIGITS = 5
AXES = ("group", "blk")
LANES = 128


def meta_digits(cluster, global_index):
    return (
        jnp.ones_like(cluster),
        cluster % BLOCK_WIDTH,
        global_index // 4096,
        (global_index // 64) % 64,
        global_index % 64,
    )


def pack_kernel(x_ref, idx_ref, cols_ref, out_ref):
    x = x_ref[...]
    squares = jnp.sum(x * x, axis=1, keepdims=True)
    unit = (x * lax.rsqrt(squares + 1e-06)).astype(jnp.bfloat16)
    row_count = x_ref.shape[0]
    slots = out_ref.shape[0]
    slot_at = lax.broadcasted_iota(jnp.int32, (slots, row_count), 0)
    picks = (slot_at == idx_ref[0:1, :]).astype(jnp.bfloat16)
    rows = jnp.dot(picks, unit, preferred_element_type=jnp.float32)
    out_ref[...] = rows.astype(jnp.bfloat16)

    cols = cols_ref[...]
    column = lax.broadcasted_iota(jnp.int32, (row_count, LANES), 1)
    spread = jnp.zeros((row_count, LANES), jnp.int32)
    for t in range(META_DIGITS):
        spread = jnp.where(column == t * CHUNK + cols[:, 0:1], cols[:, t + 1 : t + 2], spread)
    meta_picks = (slot_at == idx_ref[1:2, :]).astype(jnp.bfloat16)
    meta = jnp.dot(meta_picks, spread.astype(jnp.bfloat16), preferred_element_type=jnp.float32)
    out_ref[:, :LANES] = (rows[:, :LANES] + meta).astype(jnp.bfloat16)


def pack(embeddings, slot, meta_slot, rank, digits, slots):
    row_count, feat_width = embeddings.shape
    vmem = pltpu.MemorySpace.VMEM
    unused = jnp.zeros_like(slot)
    index_rows = jnp.stack([slot, meta_slot] + [unused] * 6, axis=0)
    cols = jnp.stack([rank, *digits] + [unused] * (7 - len(digits)), axis=1)
    return pl.pallas_call(
        pack_kernel,
        out_shape=jax.ShapeDtypeStruct((slots, feat_width), jnp.bfloat16),
        in_specs=[pl.BlockSpec(memory_space=vmem)] * 3,
        out_specs=pl.BlockSpec(memory_space=vmem),
        compiler_params=pltpu.CompilerParams(vmem_limit_bytes=48 * 1024 * 1024),
    )(embeddings, index_rows, cols)


def on_device(embeddings, cluster, global_index, send_counts):
    row_count, feat_width = embeddings.shape
    blocks = lax.axis_size("blk")
    devices = lax.axis_size("group") * blocks
    slots = devices * CHUNK
    small = lax.optimization_barrier(
        jnp.concatenate([cluster, global_index, send_counts[0]])
    )
    cluster = small[:row_count]
    global_index = small[row_count : 2 * row_count]
    counts = small[2 * row_count :]
    groups = counts.shape[0]
    upto = jnp.arange(groups)[:, None] >= jnp.arange(groups)[None, :]
    cum_ends = jnp.sum(jnp.where(upto, counts[None, :], 0), axis=1)

    position = jnp.arange(row_count, dtype=jnp.int32)
    owner_group = jnp.sum((position[:, None] >= cum_ends[None, :]).astype(jnp.int32), axis=1)
    dest = owner_group * blocks + cluster // BLOCK_WIDTH
    earlier = (dest[:, None] == dest[None, :]) & (position[None, :] < position[:, None])
    rank = jnp.sum(earlier.astype(jnp.int32), axis=1)
    slot = dest * CHUNK + rank

    send = pack(
        embeddings, slot, dest * CHUNK + CHUNK - 1, rank, meta_digits(cluster, global_index), slots
    ).reshape(devices, CHUNK, feat_width)
    slot_ids = jnp.arange(slots, dtype=jnp.int32)
    picks = slot[:, None] == slot_ids[None, :]

    got = lax.all_to_all(send, AXES, 0, 0, tiled=True)
    got_rows = got.reshape(slots, feat_width)
    coded = got[:, CHUNK - 1, : META_DIGITS * CHUNK].astype(jnp.int32)

    def digit(t):
        return coded[:, t * CHUNK : (t + 1) * CHUNK].reshape(slots)

    got_valid = digit(0) > 0
    got_sub = digit(1)
    got_ids = digit(2) * 4096 + digit(3) * 64 + digit(4)

    cosine = lax.dot_general(
        got_rows, got_rows, (((1,), (1,)), ((), ())), preferred_element_type=jnp.float32
    )
    usable = (
        got_valid[None, :]
        & (got_sub[:, None] == got_sub[None, :])
        & (got_ids[None, :] < got_ids[:, None])
    )
    best = jnp.max(jnp.where(usable, cosine, jnp.float32(-1.0)), axis=1)

    wide = jnp.pad(best.reshape(devices, CHUNK), ((0, 0), (0, LANES - CHUNK)))
    returned = lax.all_to_all(wide, AXES, 0, 0, tiled=True)[:, :CHUNK]
    return jnp.sum(jnp.where(picks, returned.reshape(1, slots), jnp.float32(0.0)), axis=1)


def solution(mesh):
    placed = (
        P(AXES, None),
        P(AXES),
        P(AXES),
        P(AXES, None),
    )
    return jax.shard_map(
        on_device, mesh=mesh, in_specs=placed, out_specs=P(AXES), check_vma=False
    )
```

```python
import jax
import jax.numpy as jnp
from jax import lax
from jax.experimental import pallas as pl
from jax.experimental.pallas import tpu as pltpu
from jax.sharding import PartitionSpec as P

BLOCK_WIDTH = 4
BLOCK_CAP = 7
CHUNK = 8
META_DIGITS = 5
AXES = ("group", "blk")
LANES = 128


def meta_digits(cluster, global_index):
    return (
        jnp.ones_like(cluster),
        cluster % BLOCK_WIDTH,
        global_index // 4096,
        (global_index // 64) % 64,
        global_index % 64,
    )


def pack_kernel(x_ref, idx_ref, cols_ref, out_ref):
    x = x_ref[...]
    squares = jnp.sum(x * x, axis=1, keepdims=True)
    unit = (x * lax.rsqrt(squares + 1e-06)).astype(jnp.bfloat16)
    row_count = x_ref.shape[0]
    slots = out_ref.shape[0]
    slot_at = lax.broadcasted_iota(jnp.int32, (slots, row_count), 0)
    picks = (slot_at == idx_ref[0:1, :]).astype(jnp.bfloat16)
    rows = jnp.dot(picks, unit, preferred_element_type=jnp.float32)
    out_ref[...] = rows.astype(jnp.bfloat16)

    cols = cols_ref[...]
    column = lax.broadcasted_iota(jnp.int32, (row_count, LANES), 1)
    spread = jnp.zeros((row_count, LANES), jnp.int32)
    for t in range(META_DIGITS):
        spread = jnp.where(column == t * CHUNK + cols[:, 0:1], cols[:, t + 1 : t + 2], spread)
    meta_picks = (slot_at == idx_ref[1:2, :]).astype(jnp.bfloat16)
    meta = jnp.dot(meta_picks, spread.astype(jnp.bfloat16), preferred_element_type=jnp.float32)
    out_ref[:, :LANES] = (rows[:, :LANES] + meta).astype(jnp.bfloat16)


def pack(embeddings, slot, meta_slot, rank, digits, slots):
    row_count, feat_width = embeddings.shape
    vmem = pltpu.MemorySpace.VMEM
    unused = jnp.zeros_like(slot)
    index_rows = jnp.stack([slot, meta_slot] + [unused] * 6, axis=0)
    cols = jnp.stack([rank, *digits] + [unused] * (7 - len(digits)), axis=1)
    return pl.pallas_call(
        pack_kernel,
        out_shape=jax.ShapeDtypeStruct((slots, feat_width), jnp.bfloat16),
        in_specs=[pl.BlockSpec(memory_space=vmem)] * 3,
        out_specs=pl.BlockSpec(memory_space=vmem),
        compiler_params=pltpu.CompilerParams(vmem_limit_bytes=48 * 1024 * 1024),
    )(embeddings, index_rows, cols)


def on_device(embeddings, cluster, global_index, send_counts):
    row_count, feat_width = embeddings.shape
    blocks = lax.axis_size("blk")
    devices = lax.axis_size("group") * blocks
    slots = devices * CHUNK
    small = lax.optimization_barrier(
        jnp.concatenate([cluster, global_index, send_counts[0]])
    )
    cluster = small[:row_count]
    global_index = small[row_count : 2 * row_count]
    counts = small[2 * row_count :]
    groups = counts.shape[0]
    upto = jnp.arange(groups)[:, None] >= jnp.arange(groups)[None, :]
    cum_ends = jnp.sum(jnp.where(upto, counts[None, :], 0), axis=1)

    position = jnp.arange(row_count, dtype=jnp.int32)
    owner_group = jnp.sum((position[:, None] >= cum_ends[None, :]).astype(jnp.int32), axis=1)
    dest = owner_group * blocks + cluster // BLOCK_WIDTH
    earlier = (dest[:, None] == dest[None, :]) & (position[None, :] < position[:, None])
    rank = jnp.sum(earlier.astype(jnp.int32), axis=1)
    slot = dest * CHUNK + rank

    send = pack(
        embeddings, slot, dest * CHUNK + CHUNK - 1, rank, meta_digits(cluster, global_index), slots
    ).reshape(devices, CHUNK, feat_width)
    slot_ids = jnp.arange(slots, dtype=jnp.int32)
    picks = slot_ids[:, None] == slot[None, :]

    got = lax.all_to_all(send, AXES, 0, 0, tiled=True)
    got_rows = got.reshape(slots, feat_width)
    coded = got[:, CHUNK - 1, : META_DIGITS * CHUNK].astype(jnp.int32)

    def digit(t):
        return coded[:, t * CHUNK : (t + 1) * CHUNK]

    packed = (
        (digit(2) * 4096 + digit(3) * 64 + digit(4)) * 8 + digit(1) * 2 + digit(0)
    ).reshape(slots)
    got_valid = (packed & 1) > 0
    got_sub = (packed >> 1) & 3
    got_ids = packed >> 3

    cosine = lax.dot_general(
        got_rows, got_rows, (((1,), (1,)), ((), ())), preferred_element_type=jnp.float32
    )
    usable = (
        got_valid[None, :]
        & (got_sub[:, None] == got_sub[None, :])
        & (got_ids[None, :] < got_ids[:, None])
    )
    best = jnp.max(jnp.where(usable, cosine, jnp.float32(-1.0)), axis=1)

    wide = jnp.pad(best.reshape(devices, CHUNK), ((0, 0), (0, LANES - CHUNK)))
    returned = lax.all_to_all(wide, AXES, 0, 0, tiled=True)[:, :CHUNK]
    return jnp.sum(jnp.where(picks, returned.reshape(slots, 1), jnp.float32(0.0)), axis=0)


def solution(mesh):
    placed = (
        P(AXES, None),
        P(AXES),
        P(AXES),
        P(AXES, None),
    )
    return jax.shard_map(
        on_device, mesh=mesh, in_specs=placed, out_specs=P(AXES), check_vma=False
    )
```

```python
import jax
import jax.numpy as jnp
from jax import lax
from jax.experimental import pallas as pl
from jax.experimental.pallas import tpu as pltpu
from jax.sharding import PartitionSpec as P

BLOCK_WIDTH = 4
BLOCK_CAP = 7
CHUNK = 8
META_DIGITS = 5
AXES = ("group", "blk")
LANES = 128
VMEM_LIMIT = 50 * 1024 * 1024


def meta_digits(cluster, global_index):
    return (
        jnp.ones_like(cluster),
        cluster % BLOCK_WIDTH,
        global_index // 4096,
        (global_index // 64) % 64,
        global_index % 64,
    )


def pack_kernel(x_hbm, idx_ref, cols_ref, out_ref, x_buf, unit_buf, sems):
    pieces = sems.shape[0]
    piece = x_buf.shape[0] // pieces
    copies = [
        pltpu.make_async_copy(
            x_hbm.at[pl.ds(j * piece, piece)], x_buf.at[pl.ds(j * piece, piece)], sems.at[j]
        )
        for j in range(pieces)
    ]
    for copy in copies:
        copy.start()
    row_count = x_buf.shape[0]
    slots = out_ref.shape[0]

    cols = cols_ref[...]
    column = lax.broadcasted_iota(jnp.int32, (row_count, LANES), 1)
    spread = jnp.zeros((row_count, LANES), jnp.int32)
    for t in range(META_DIGITS):
        spread = jnp.where(column == t * CHUNK + cols[:, 0:1], cols[:, t + 1 : t + 2], spread)
    slot_at = lax.broadcasted_iota(jnp.int32, (slots, row_count), 0)
    meta_picks = (slot_at == idx_ref[1:2, :]).astype(jnp.bfloat16)
    meta = jnp.dot(meta_picks, spread.astype(jnp.bfloat16), preferred_element_type=jnp.float32)
    picks = (slot_at == idx_ref[0:1, :]).astype(jnp.bfloat16)

    for j, copy in enumerate(copies):
        copy.wait()
        x = x_buf[pl.ds(j * piece, piece), :]
        squares = jnp.sum(x * x, axis=1, keepdims=True)
        unit_buf[pl.ds(j * piece, piece), :] = (x * lax.rsqrt(squares + 1e-06)).astype(jnp.bfloat16)
    rows = jnp.dot(picks, unit_buf[...], preferred_element_type=jnp.float32)
    out_ref[...] = rows.astype(jnp.bfloat16)
    out_ref[:, :LANES] = (rows[:, :LANES] + meta).astype(jnp.bfloat16)


def pack(embeddings, slot, meta_slot, rank, digits, slots):
    row_count, feat_width = embeddings.shape
    vmem = pltpu.MemorySpace.VMEM
    unused = jnp.zeros_like(slot)
    index_rows = jnp.stack([slot, meta_slot] + [unused] * 6, axis=0)
    cols = jnp.stack([rank, *digits] + [unused] * (7 - len(digits)), axis=1)
    return pl.pallas_call(
        pack_kernel,
        out_shape=jax.ShapeDtypeStruct((slots, feat_width), jnp.bfloat16),
        in_specs=[pl.BlockSpec(memory_space=pl.ANY)] + [pl.BlockSpec(memory_space=vmem)] * 2,
        out_specs=pl.BlockSpec(memory_space=vmem),
        scratch_shapes=[
            pltpu.VMEM((row_count, feat_width), jnp.float32),
            pltpu.VMEM((row_count, feat_width), jnp.bfloat16),
            pltpu.SemaphoreType.DMA((4,)),
        ],
        compiler_params=pltpu.CompilerParams(vmem_limit_bytes=VMEM_LIMIT),
    )(embeddings, index_rows, cols)


def on_device(embeddings, cluster, global_index, send_counts):
    row_count, feat_width = embeddings.shape
    blocks = lax.axis_size("blk")
    devices = lax.axis_size("group") * blocks
    slots = devices * CHUNK
    small = lax.optimization_barrier(
        jnp.concatenate([cluster, global_index, send_counts[0]])
    )
    cluster = small[:row_count]
    global_index = small[row_count : 2 * row_count]
    counts = small[2 * row_count :]
    groups = counts.shape[0]
    upto = jnp.arange(groups)[:, None] >= jnp.arange(groups)[None, :]
    cum_ends = jnp.sum(jnp.where(upto, counts[None, :], 0), axis=1)

    position = jnp.arange(row_count, dtype=jnp.int32)
    owner_group = jnp.sum((position[:, None] >= cum_ends[None, :]).astype(jnp.int32), axis=1)
    dest = owner_group * blocks + cluster // BLOCK_WIDTH
    earlier = (dest[:, None] == dest[None, :]) & (position[None, :] < position[:, None])
    rank = jnp.sum(earlier.astype(jnp.int32), axis=1)
    slot = dest * CHUNK + rank

    send = pack(
        embeddings, slot, dest * CHUNK + CHUNK - 1, rank, meta_digits(cluster, global_index), slots
    ).reshape(devices, CHUNK, feat_width)
    slot_ids = jnp.arange(slots, dtype=jnp.int32)
    picks = slot_ids[:, None] == slot[None, :]

    got = lax.all_to_all(send, AXES, 0, 0, tiled=True)
    got_rows = got.reshape(slots, feat_width)
    coded = got[:, CHUNK - 1, : META_DIGITS * CHUNK].astype(jnp.int32)

    def digit(t):
        return coded[:, t * CHUNK : (t + 1) * CHUNK].reshape(slots)

    got_valid = digit(0) > 0
    got_sub = digit(1)
    got_ids = digit(2) * 4096 + digit(3) * 64 + digit(4)

    cosine = lax.dot_general(
        got_rows, got_rows, (((1,), (1,)), ((), ())), preferred_element_type=jnp.float32
    )
    usable = (
        got_valid[None, :]
        & (got_sub[:, None] == got_sub[None, :])
        & (got_ids[None, :] < got_ids[:, None])
    )
    best = jnp.max(jnp.where(usable, cosine, jnp.float32(-1.0)), axis=1)

    wide = jnp.pad(best.reshape(devices, CHUNK), ((0, 0), (0, LANES - CHUNK)))
    returned = lax.all_to_all(wide, AXES, 0, 0, tiled=True)[:, :CHUNK]
    return jnp.sum(jnp.where(picks, returned.reshape(slots, 1), jnp.float32(0.0)), axis=0)


def solution(mesh):
    placed = (
        P(AXES, None),
        P(AXES),
        P(AXES),
        P(AXES, None),
    )
    return jax.shard_map(
        on_device, mesh=mesh, in_specs=placed, out_specs=P(AXES), check_vma=False
    )
```

```python
import jax
import jax.numpy as jnp
from jax import lax
from jax.experimental import pallas as pl
from jax.experimental.pallas import tpu as pltpu
from jax.sharding import PartitionSpec as P

BLOCK_WIDTH = 4
BLOCK_CAP = 7
CHUNK = 8
META_DIGITS = 5
AXES = ("group", "blk")
LANES = 128


def meta_digits(cluster, global_index):
    return (
        jnp.ones_like(cluster),
        cluster % BLOCK_WIDTH,
        global_index // 4096,
        (global_index // 64) % 64,
        global_index % 64,
    )


def pack_kernel(x_ref, idx_ref, cols_ref, out_ref):
    x = x_ref[...]
    squares = jnp.sum(x * x, axis=1, keepdims=True)
    unit = (x * lax.rsqrt(squares + 1e-06)).astype(jnp.bfloat16)
    row_count = x_ref.shape[0]
    slots = out_ref.shape[0]
    slot_at = lax.broadcasted_iota(jnp.int32, (slots, row_count), 0)
    picks = (slot_at == idx_ref[0:1, :]).astype(jnp.bfloat16)
    rows = jnp.dot(picks, unit, preferred_element_type=jnp.float32)
    out_ref[:, LANES:] = rows[:, LANES:].astype(jnp.bfloat16)

    cols = cols_ref[...]
    column = lax.broadcasted_iota(jnp.int32, (row_count, LANES), 1)
    spread = jnp.zeros((row_count, LANES), jnp.int32)
    for t in range(META_DIGITS):
        spread = jnp.where(column == t * CHUNK + cols[:, 0:1], cols[:, t + 1 : t + 2], spread)
    meta_picks = (slot_at == idx_ref[1:2, :]).astype(jnp.bfloat16)
    meta = jnp.dot(meta_picks, spread.astype(jnp.bfloat16), preferred_element_type=jnp.float32)
    out_ref[:, :LANES] = (rows[:, :LANES] + meta).astype(jnp.bfloat16)


def pack(embeddings, slot, meta_slot, rank, digits, slots):
    row_count, feat_width = embeddings.shape
    vmem = pltpu.MemorySpace.VMEM
    unused = jnp.zeros_like(slot)
    index_rows = jnp.stack([slot, meta_slot] + [unused] * 6, axis=0)
    cols = jnp.stack([rank, *digits] + [unused] * (7 - len(digits)), axis=1)
    return pl.pallas_call(
        pack_kernel,
        out_shape=jax.ShapeDtypeStruct((slots, feat_width), jnp.bfloat16),
        in_specs=[pl.BlockSpec(memory_space=vmem)] * 3,
        out_specs=pl.BlockSpec(memory_space=vmem),
        compiler_params=pltpu.CompilerParams(vmem_limit_bytes=48 * 1024 * 1024),
    )(embeddings, index_rows, cols)


def on_device(embeddings, cluster, global_index, send_counts):
    row_count, feat_width = embeddings.shape
    blocks = lax.axis_size("blk")
    devices = lax.axis_size("group") * blocks
    slots = devices * CHUNK
    small = lax.optimization_barrier(
        jnp.concatenate([cluster, global_index, send_counts[0]])
    )
    cluster = small[:row_count]
    global_index = small[row_count : 2 * row_count]
    counts = small[2 * row_count :]
    groups = counts.shape[0]
    upto = jnp.arange(groups)[:, None] >= jnp.arange(groups)[None, :]
    cum_ends = jnp.sum(jnp.where(upto, counts[None, :], 0), axis=1)

    position = jnp.arange(row_count, dtype=jnp.int32)
    owner_group = jnp.sum((position[:, None] >= cum_ends[None, :]).astype(jnp.int32), axis=1)
    dest = owner_group * blocks + cluster // BLOCK_WIDTH
    earlier = (dest[:, None] == dest[None, :]) & (position[None, :] < position[:, None])
    rank = jnp.sum(earlier.astype(jnp.int32), axis=1)
    slot = dest * CHUNK + rank

    send = pack(
        embeddings, slot, dest * CHUNK + CHUNK - 1, rank, meta_digits(cluster, global_index), slots
    ).reshape(devices, CHUNK, feat_width)
    slot_ids = jnp.arange(slots, dtype=jnp.int32)
    picks = slot_ids[:, None] == slot[None, :]

    got = lax.all_to_all(send, AXES, 0, 0, tiled=True)
    got_rows = got.reshape(slots, feat_width)
    coded = got[:, CHUNK - 1, : META_DIGITS * CHUNK].astype(jnp.int32)

    def digit(t):
        return coded[:, t * CHUNK : (t + 1) * CHUNK].reshape(slots)

    got_valid = digit(0) > 0
    got_sub = digit(1)
    got_ids = digit(2) * 4096 + digit(3) * 64 + digit(4)

    cosine = lax.dot_general(
        got_rows, got_rows, (((1,), (1,)), ((), ())), preferred_element_type=jnp.float32
    )
    usable = (
        got_valid[None, :]
        & (got_sub[:, None] == got_sub[None, :])
        & (got_ids[None, :] < got_ids[:, None])
    )
    best = jnp.max(jnp.where(usable, cosine, jnp.float32(-1.0)), axis=1)

    wide = jnp.pad(best.reshape(devices, CHUNK), ((0, 0), (0, LANES - CHUNK)))
    returned = lax.all_to_all(wide, AXES, 0, 0, tiled=True)[:, :CHUNK]
    return jnp.sum(jnp.where(picks, returned.reshape(slots, 1), jnp.float32(0.0)), axis=0)


def solution(mesh):
    placed = (
        P(AXES, None),
        P(AXES),
        P(AXES),
        P(AXES, None),
    )
    return jax.shard_map(
        on_device, mesh=mesh, in_specs=placed, out_specs=P(AXES), check_vma=False
    )
```

```python
import jax
import jax.numpy as jnp
from jax import lax
from jax.experimental import pallas as pl
from jax.experimental.pallas import tpu as pltpu
from jax.sharding import PartitionSpec as P

BLOCK_WIDTH = 4
BLOCK_CAP = 7
CHUNK = 8
META_DIGITS = 5
AXES = ("group", "blk")
LANES = 128


def meta_digits(cluster, global_index):
    return (
        jnp.ones_like(cluster),
        cluster % BLOCK_WIDTH,
        global_index // 4096,
        (global_index // 64) % 64,
        global_index % 64,
    )


def pack_kernel(x_ref, idx_ref, cols_ref, out_ref):
    x = x_ref[...]
    squares = jnp.sum(x * x, axis=1, keepdims=True)
    unit = (x * lax.rsqrt(squares + 1e-06)).astype(jnp.bfloat16)
    row_count = x_ref.shape[0]
    slots = out_ref.shape[0]
    slot_at = lax.broadcasted_iota(jnp.int32, (slots, row_count), 0)
    picks = (slot_at == idx_ref[0:1, :]).astype(jnp.bfloat16)
    rows = jnp.dot(picks, unit, preferred_element_type=jnp.float32)
    out_ref[...] = rows.astype(jnp.bfloat16)

    cols = cols_ref[...]
    column = lax.broadcasted_iota(jnp.int32, (row_count, LANES), 1)
    spread = jnp.zeros((row_count, LANES), jnp.int32)
    for t in range(META_DIGITS):
        spread = jnp.where(column == t * CHUNK + cols[:, 0:1], cols[:, t + 1 : t + 2], spread)
    meta_picks = (slot_at == idx_ref[1:2, :]).astype(jnp.bfloat16)
    meta = jnp.dot(meta_picks, spread.astype(jnp.bfloat16), preferred_element_type=jnp.float32)
    out_ref[:, :LANES] = (rows[:, :LANES] + meta).astype(jnp.bfloat16)


def pack(embeddings, slot, meta_slot, rank, digits, slots):
    row_count, feat_width = embeddings.shape
    vmem = pltpu.MemorySpace.VMEM
    unused = jnp.zeros_like(slot)
    index_rows = jnp.stack([slot, meta_slot] + [unused] * 6, axis=0)
    cols = jnp.stack([rank, *digits] + [unused] * (7 - len(digits)), axis=1)
    return pl.pallas_call(
        pack_kernel,
        out_shape=jax.ShapeDtypeStruct((slots, feat_width), jnp.bfloat16),
        in_specs=[pl.BlockSpec(memory_space=vmem)] * 3,
        out_specs=pl.BlockSpec(memory_space=vmem),
        compiler_params=pltpu.CompilerParams(vmem_limit_bytes=48 * 1024 * 1024),
    )(embeddings, index_rows, cols)


def on_device(embeddings, cluster, global_index, send_counts):
    row_count, feat_width = embeddings.shape
    blocks = lax.axis_size("blk")
    devices = lax.axis_size("group") * blocks
    slots = devices * CHUNK
    small = lax.optimization_barrier(
        jnp.concatenate([cluster, global_index, send_counts[0]])
    )
    cluster = small[:row_count]
    global_index = small[row_count : 2 * row_count]
    counts = small[2 * row_count :]
    groups = counts.shape[0]
    upto = jnp.arange(groups)[:, None] >= jnp.arange(groups)[None, :]
    cum_ends = jnp.sum(jnp.where(upto, counts[None, :], 0), axis=1)

    position = jnp.arange(row_count, dtype=jnp.int32)
    owner_group = jnp.sum((position[:, None] >= cum_ends[None, :]).astype(jnp.int32), axis=1)
    dest = owner_group * blocks + cluster // BLOCK_WIDTH
    earlier = (dest[:, None] == dest[None, :]) & (position[None, :] < position[:, None])
    rank = jnp.sum(earlier.astype(jnp.int32), axis=1)
    slot = dest * CHUNK + rank

    send = pack(
        embeddings, slot, dest * CHUNK + CHUNK - 1, rank, meta_digits(cluster, global_index), slots
    ).reshape(devices, CHUNK, feat_width)
    slot_ids = jnp.arange(slots, dtype=jnp.int32)
    picks = slot_ids[:, None] == slot[None, :]

    got = lax.all_to_all(send, AXES, 0, 0, tiled=True)
    got_rows = got.reshape(slots, feat_width)
    coded = got[:, CHUNK - 1, : META_DIGITS * CHUNK].astype(jnp.int32)

    def digit(t):
        return coded[:, t * CHUNK : (t + 1) * CHUNK].reshape(slots)

    got_valid = digit(0) > 0
    got_sub = digit(1)
    got_ids = digit(2) * 4096 + digit(3) * 64 + digit(4)

    cosine = lax.dot_general(
        got_rows, got_rows, (((1,), (1,)), ((), ())), preferred_element_type=jnp.float32
    )
    key = jnp.where(got_valid, got_sub * 131072 + got_ids, 1 << 30)
    gap = key[:, None] - key[None, :]
    usable = (gap > 0) & (gap <= got_ids[:, None])
    best = jnp.max(jnp.where(usable, cosine, jnp.float32(-1.0)), axis=1)

    wide = jnp.pad(best.reshape(devices, CHUNK), ((0, 0), (0, LANES - CHUNK)))
    returned = lax.all_to_all(wide, AXES, 0, 0, tiled=True)[:, :CHUNK]
    return jnp.sum(jnp.where(picks, returned.reshape(slots, 1), jnp.float32(0.0)), axis=0)


def solution(mesh):
    placed = (
        P(AXES, None),
        P(AXES),
        P(AXES),
        P(AXES, None),
    )
    return jax.shard_map(
        on_device, mesh=mesh, in_specs=placed, out_specs=P(AXES), check_vma=False
    )
```

```python
import jax
import jax.numpy as jnp
from jax import lax
from jax.experimental import pallas as pl
from jax.experimental.pallas import tpu as pltpu
from jax.sharding import PartitionSpec as P

BLOCK_WIDTH = 4
BLOCK_CAP = 7
CHUNK = 8
META_DIGITS = 5
AXES = ("group", "blk")
LANES = 128


def meta_digits(cluster, global_index):
    return (
        jnp.ones_like(cluster),
        cluster % BLOCK_WIDTH,
        global_index // 4096,
        (global_index // 64) % 64,
        global_index % 64,
    )


def pack_kernel(x_ref, idx_ref, cols_ref, out_ref):
    x = x_ref[...]
    squares = jnp.sum(x * x, axis=1, keepdims=True)
    unit = (x * lax.rsqrt(squares + 1e-06)).astype(jnp.bfloat16)
    row_count = x_ref.shape[0]
    slots = out_ref.shape[0]
    slot_at = lax.broadcasted_iota(jnp.int32, (slots, row_count), 0)
    picks = (slot_at == idx_ref[0:1, :]).astype(jnp.bfloat16)
    rows = jnp.dot(picks, unit, preferred_element_type=jnp.float32)
    out_ref[...] = rows.astype(jnp.bfloat16)

    cols = cols_ref[...]
    column = lax.broadcasted_iota(jnp.int32, (row_count, LANES), 1)
    spread = jnp.zeros((row_count, LANES), jnp.int32)
    for t in range(META_DIGITS):
        spread = jnp.where(column == t * CHUNK + cols[:, 0:1], cols[:, t + 1 : t + 2], spread)
    meta_picks = (slot_at == idx_ref[1:2, :]).astype(jnp.bfloat16)
    meta = jnp.dot(meta_picks, spread.astype(jnp.bfloat16), preferred_element_type=jnp.float32)
    out_ref[:, :LANES] = (rows[:, :LANES] + meta).astype(jnp.bfloat16)


def pack(embeddings, slot, meta_slot, rank, digits, slots):
    row_count, feat_width = embeddings.shape
    vmem = pltpu.MemorySpace.VMEM
    unused = jnp.zeros_like(slot)
    index_rows = jnp.stack([slot, meta_slot] + [unused] * 6, axis=0)
    cols = jnp.stack([rank, *digits] + [unused] * (7 - len(digits)), axis=1)
    return pl.pallas_call(
        pack_kernel,
        out_shape=jax.ShapeDtypeStruct((slots, feat_width), jnp.bfloat16),
        in_specs=[pl.BlockSpec(memory_space=vmem)] * 3,
        out_specs=pl.BlockSpec(memory_space=vmem),
        compiler_params=pltpu.CompilerParams(vmem_limit_bytes=48 * 1024 * 1024),
    )(embeddings, index_rows, cols)


def on_device(embeddings, cluster, global_index, send_counts):
    row_count, feat_width = embeddings.shape
    blocks = lax.axis_size("blk")
    devices = lax.axis_size("group") * blocks
    slots = devices * CHUNK
    small = lax.optimization_barrier(
        jnp.concatenate([cluster, global_index, send_counts[0]])
    )
    cluster = small[:row_count]
    global_index = small[row_count : 2 * row_count]
    counts = small[2 * row_count :]
    groups = counts.shape[0]
    upto = jnp.arange(groups)[:, None] >= jnp.arange(groups)[None, :]
    cum_ends = jnp.sum(jnp.where(upto, counts[None, :], 0), axis=1)

    position = jnp.arange(row_count, dtype=jnp.int32)
    owner_group = jnp.sum((position[:, None] >= cum_ends[None, :]).astype(jnp.int32), axis=1)
    dest = owner_group * blocks + cluster // BLOCK_WIDTH
    earlier = (dest[:, None] == dest[None, :]) & (position[None, :] < position[:, None])
    rank = jnp.sum(earlier.astype(jnp.int32), axis=1)
    slot = dest * CHUNK + rank

    send = pack(
        embeddings, slot, dest * CHUNK + CHUNK - 1, rank, meta_digits(cluster, global_index), slots
    ).reshape(devices, CHUNK, feat_width)
    slot_ids = jnp.arange(slots, dtype=jnp.int32)
    picks = slot_ids[:, None] == slot[None, :]

    got = lax.all_to_all(send, AXES, 0, 0, tiled=True)
    got_rows = got.reshape(slots, feat_width)
    coded = got[:, CHUNK - 1, : META_DIGITS * CHUNK].astype(jnp.int32)

    def digit(t):
        return coded[:, t * CHUNK : (t + 1) * CHUNK].reshape(slots)

    got_valid = digit(0) > 0
    got_sub = digit(1)
    got_ids = digit(2) * 4096 + digit(3) * 64 + digit(4)

    cosine = lax.dot_general(
        got_rows, got_rows, (((1,), (1,)), ((), ())), preferred_element_type=jnp.float32
    )
    key = jnp.where(got_valid, got_sub * 131072 + got_ids, 1 << 30)
    gap = key[:, None] - key[None, :]
    usable = (gap > 0) & (gap <= (key & 131071)[:, None])
    best = jnp.max(jnp.where(usable, cosine, jnp.float32(-1.0)), axis=1)

    wide = jnp.pad(best.reshape(devices, CHUNK), ((0, 0), (0, LANES - CHUNK)))
    returned = lax.all_to_all(wide, AXES, 0, 0, tiled=True)[:, :CHUNK]
    return jnp.sum(jnp.where(picks, returned.reshape(slots, 1), jnp.float32(0.0)), axis=0)


def solution(mesh):
    placed = (
        P(AXES, None),
        P(AXES),
        P(AXES),
        P(AXES, None),
    )
    return jax.shard_map(
        on_device, mesh=mesh, in_specs=placed, out_specs=P(AXES), check_vma=False
    )
```
